256 devices in a mesh: section: 2 (over y_lo), dp: 4 (over x), tensor: 32 (over z, y_hi, core).
Axes of the slice: x: 4, y: 4 (y_hi: 2, y_lo: 2; y = y_hi * 2 + y_lo), z: 8, core: 2. Of those that a mesh axis runs over, the one named last changes fastest.
Arguments:
- inputs: bfloat16 [2, 1024, 12288], P('section', 'dp', 'tensor'), may hold values from -6 to 6
- queries: bfloat16 [2, 1024, 8192], P('section', 'dp', 'tensor'), may hold values from -8 to 8
- keys: bfloat16 [2, 1024, 8192], P('section', 'dp', 'tensor'), may hold values from -8 to 8
- w_value: bfloat16 [2, 12288, 8192], P('section', None, 'tensor'), may hold values from -0.0546875 to 0.0546875
- w_out: bfloat16 [2, 8192, 12288], P('section', 'tensor'), may hold values from -0.75 to 0.75
Outputs:
- next_inputs: bfloat16 [2, 1024, 12288], P('section', 'dp', 'tensor')
The draws below stay inside these ranges and needn't reach their ends.
All inputs are finite; a program needn't handle non-finite values.
Results may differ from the reference program's by a relative error of at most 0.023.
Values may be sent and summed in bfloat16 or wider, within the bound.
No kernel may reach another device: no remote copies, remote signals or barrier semaphores. Data moves between devices by JAX's collectives and lax.ppermute only.
A program may use at most 64 MiB of HBM per device.

```python
import jax
import jax.numpy as jnp
from jax import lax

D = 12288
HEAD_SIZE = 128
HEAD_DEV = 2
LEN = 256
HEADS = 64
TOKENS = 1024
N_DP = 4
N_TENSOR = 32


def draw_queries(key, part):
    shape = (2, TOKENS, HEADS * HEAD_SIZE)
    return jnp.clip(jax.random.normal(jax.random.fold_in(key, 11), shape, jnp.float32), -4.0, 4.0).astype(jnp.bfloat16)


def draw_keys(key, part):
    shape = (2, TOKENS, HEADS * HEAD_SIZE)
    return jnp.clip(jax.random.normal(jax.random.fold_in(key, 13), shape, jnp.float32), -4.0, 4.0).astype(jnp.bfloat16)


def raised(entries, own_key, source, target, blocks, factor):
    owner, partner = [(jnp.arange(entries.shape[axis_at]) // (entries.shape[axis_at] // blocks)).reshape([-1 if axis == axis_at else 1 for axis in range(entries.ndim)]) for axis_at in (source, target)]
    chosen = jax.random.permutation(own_key, blocks)[partner]
    strong = (owner == chosen) | (owner == (partner + blocks // 2) % blocks)
    return jnp.where(strong, factor * entries, entries)


def block_scale(own_key, extent, shards, least, high):
    loudness, own = 1.0, jax.random.fold_in(own_key, 6)
    for dim, blocks in shards:
        heights = jnp.exp(jax.random.uniform(jax.random.fold_in(own, dim), (blocks,), jnp.float32, least / len(shards), high / len(shards)))
        loudness = loudness * jnp.repeat(heights, extent[dim] // blocks).reshape([-1 if axis == dim else 1 for axis in range(len(extent))])
    return loudness


def centred(key, extent, spread, bound, split=(), dtype=jnp.bfloat16):
    level = block_scale(key, extent, split, -0.22, 0.18) if split else 1.0
    values = jax.random.normal(key, extent, jnp.float32) * spread * level
    return jnp.minimum(jnp.maximum(values, -bound), bound).astype(dtype)


def gaussian_with(own_key, extent, width, reach, cuts, heavy, dtype=jnp.bfloat16):
    result = width * jax.random.normal(own_key, extent, jnp.float32)
    if cuts:
        result = result * block_scale(own_key, extent, cuts, -0.22, 0.18)
    return jnp.clip(raised(result, jax.random.fold_in(own_key, 3), *heavy), -reach, reach).astype(dtype)


def setup_inputs(seed: int = 0) -> dict:
    seeds = jax.random.split(jax.random.key(seed), 6)
    return {
        "inputs": centred(seeds[0], (2, TOKENS, D), 1.0, 6.0, ((0, 2), (1, 4), (2, 32))),
        "queries": draw_queries(jax.random.fold_in(seeds[5], 71), 0),
        "keys": draw_keys(jax.random.fold_in(seeds[5], 71), 0),
        "w_value": centred(seeds[3], (2, D, HEADS * HEAD_SIZE), D ** -0.5, 0.0546875, ((0, 2), (2, 32))),
        "w_out": gaussian_with(seeds[4], (2, HEADS * HEAD_SIZE, D), (HEAD_DEV * HEAD_SIZE) ** -0.5, 0.75, ((0, 2), (1, 32)), (1, 2, 32, 2.75)),
    }


def attend_one(parts):
    query_rows, key_rows, value_rows = parts
    scores = jnp.einsum('qhd,khd->hqk', query_rows.astype(jnp.float32), key_rows.astype(jnp.float32)) / jnp.sqrt(jnp.float32(HEAD_SIZE))
    rows = lax.broadcasted_iota(jnp.int32, (LEN, LEN), 0)
    cols = lax.broadcasted_iota(jnp.int32, (LEN, LEN), 1)
    scores = jnp.where((cols <= rows)[None], scores, jnp.float32(-1e+30))
    top = lax.optimization_barrier(jnp.max(scores, axis=-1, keepdims=True))
    expo = jnp.exp(scores - top)
    probs = (expo / lax.optimization_barrier(jnp.sum(expo, axis=-1, keepdims=True))).astype(jnp.bfloat16)
    return jnp.einsum('hqk,khd->qhd', probs.astype(jnp.float32), value_rows.astype(jnp.float32)).astype(jnp.bfloat16)

def block(activ, query_all, key_all, weight_v, weight_o):
    values = jnp.dot(activ, weight_v, preferred_element_type=jnp.float32).astype(jnp.bfloat16)
    shape4 = (N_DP, LEN, HEADS, HEAD_SIZE)
    context = lax.map(attend_one, (query_all.reshape(shape4), key_all.reshape(shape4), values.reshape(shape4)))
    group_dim = HEAD_DEV * HEAD_SIZE
    context = context.reshape(TOKENS, N_TENSOR, group_dim).transpose(1, 0, 2)
    weight_groups = weight_o.reshape(N_TENSOR, group_dim, D)

    def add_group(total, pair):
        term = jnp.dot(pair[0], pair[1], preferred_element_type=jnp.float32).astype(jnp.bfloat16)
        term = lax.optimization_barrier(term)
        return (total + term.astype(jnp.float32), None)
    total, unused = lax.scan(add_group, jnp.zeros((TOKENS, D), jnp.float32), (context, weight_groups))
    return (total + activ.astype(jnp.float32)).astype(jnp.bfloat16)

def reference(inputs, queries, keys, w_value, w_out):
    first = block(inputs[0], queries[0], keys[0], w_value[0], w_out[0])
    second = block(inputs[1], queries[1], keys[1], w_value[1], w_out[1])
    return jnp.stack([second, first])
```

```python
import jax
import jax.numpy as jnp
from jax import lax
from jax.sharding import Mesh
from jax.sharding import PartitionSpec as P

HEAD_SIZE = 128
LEN = 256
N_Z, N_Y, N_C = 8, 2, 2


def on_device(inputs, queries, keys, w_value, w_out):
    activ = inputs[0]
    weight_v = w_value[0]
    weight_o = w_out[0]
    length = activ.shape[0]
    col_width = activ.shape[1]
    n_feat = weight_v.shape[0]

    gathered = lax.all_gather(activ, "ty", axis=0)
    gathered = lax.all_gather(gathered, "tz", axis=0)
    gathered = lax.all_gather(gathered, "tc", axis=0)
    wv = weight_v.reshape(N_Z, N_Y, N_C, col_width, weight_v.shape[1])
    values = jnp.einsum(
        "czytf,zycfh->th", gathered, wv, preferred_element_type=jnp.float32
    ).astype(jnp.bfloat16)

    heads_here = weight_v.shape[1] // HEAD_SIZE
    query_rows = queries[0].reshape(length // LEN, LEN, heads_here, HEAD_SIZE)
    key_rows = keys[0].reshape(length // LEN, LEN, heads_here, HEAD_SIZE)
    value_rows = values.reshape(length // LEN, LEN, heads_here, HEAD_SIZE)
    scores = jnp.einsum(
        "bqhd,bkhd->bhqk", query_rows, key_rows, preferred_element_type=jnp.float32
    ) / jnp.sqrt(jnp.float32(HEAD_SIZE))
    rows = lax.broadcasted_iota(jnp.int32, (LEN, LEN), 0)
    cols = lax.broadcasted_iota(jnp.int32, (LEN, LEN), 1)
    scores = jnp.where((cols <= rows)[None, None], scores, jnp.float32(-1e30))
    top = jnp.max(scores, axis=-1, keepdims=True)
    expo = jnp.exp(scores - top)
    probs = (expo / jnp.sum(expo, axis=-1, keepdims=True)).astype(jnp.bfloat16)
    context = jnp.einsum(
        "bhqk,bkhd->bqhd", probs, value_rows, preferred_element_type=jnp.float32
    ).astype(jnp.bfloat16)
    context = context.reshape(length, heads_here * HEAD_SIZE)

    wo = weight_o.reshape(weight_o.shape[0], N_Z, N_Y, N_C, col_width)
    partial_term = jnp.einsum(
        "tk,kzycf->czytf", context, wo, preferred_element_type=jnp.float32
    ).astype(jnp.bfloat16)
    part = lax.psum_scatter(partial_term, "tc", scatter_dimension=0, tiled=False)
    part = lax.psum_scatter(part, "tz", scatter_dimension=0, tiled=False)
    part = lax.psum_scatter(part, "ty", scatter_dimension=0, tiled=False)
    result = (part.astype(jnp.float32) + activ.astype(jnp.float32)).astype(jnp.bfloat16)
    passed = lax.ppermute(result, "section", [(0, 1), (1, 0)])
    return passed[None]


def solution(mesh):
    n_sec, n_dp, n_t = mesh.devices.shape
    sub = Mesh(
        mesh.devices.reshape(n_sec, n_dp, N_Z, N_Y, N_C),
        ("section", "dp", "tz", "ty", "tc"),
    )
    spec = P("section", "dp", ("tz", "ty", "tc"))
    return jax.shard_map(
        on_device,
        mesh=sub,
        in_specs=(
            spec,
            spec,
            spec,
            P("section", None, ("tz", "ty", "tc")),
            P("section", ("tz", "ty", "tc"), None),
        ),
        out_specs=spec,
        check_vma=False,
    )
```

```python
import jax
import jax.numpy as jnp
from jax import lax
from jax.experimental import pallas as pl
from jax.experimental.pallas import tpu as pltpu
from jax.sharding import Mesh
from jax.sharding import PartitionSpec as P

HEAD_SIZE = 128
LEN = 256
N_Z, N_Y, N_C = 8, 2, 2
GROUPS_PER_STEP = 4


def swap(value, axis):
    return lax.ppermute(value, axis, [(0, 1), (1, 0)])


def out_proj_kernel(core_ref, ctx_ref, w_ref, mine_ref, sib_ref):
    width = mine_ref.shape[2]
    is_zero = core_ref[0] == 0
    ctx = ctx_ref[...]
    for i in range(mine_ref.shape[0]):
        lo = i * 2 * width
        d0 = jnp.dot(ctx, w_ref[:, lo:lo + width], preferred_element_type=jnp.float32)
        d1 = jnp.dot(ctx, w_ref[:, lo + width:lo + 2 * width], preferred_element_type=jnp.float32)
        d0 = d0.astype(jnp.bfloat16)
        d1 = d1.astype(jnp.bfloat16)
        mine_ref[i] = jnp.where(is_zero, d0, d1)
        sib_ref[i] = jnp.where(is_zero, d1, d0)


def out_proj(core, context, weight_o, width):
    tokens, inner = context.shape
    n_groups = weight_o.shape[1] // (N_C * width)
    step = GROUPS_PER_STEP
    out = jax.ShapeDtypeStruct((n_groups, tokens, width), jnp.bfloat16)
    return pl.pallas_call(
        out_proj_kernel,
        out_shape=(out, out),
        grid_spec=pltpu.PrefetchScalarGridSpec(
            num_scalar_prefetch=1,
            grid=(n_groups // step,),
            in_specs=[
                pl.BlockSpec((tokens, inner), lambda i, c: (0, 0)),
                pl.BlockSpec((inner, step * N_C * width), lambda i, c: (0, i)),
            ],
            out_specs=[
                pl.BlockSpec((step, tokens, width), lambda i, c: (i, 0, 0)),
                pl.BlockSpec((step, tokens, width), lambda i, c: (i, 0, 0)),
            ],
        ),
    )(core, context, weight_o)


def on_device(inputs, queries, keys, w_value, w_out):
    activ = inputs[0]
    weight_v = w_value[0]
    weight_o = w_out[0]
    length = activ.shape[0]
    col_width = activ.shape[1]
    n_feat = weight_v.shape[0]

    y_first = lax.axis_index("ty") == 0
    other = swap(activ, "ty")
    gathered = jnp.stack([jnp.where(y_first, activ, other), jnp.where(y_first, other, activ)])
    gathered = lax.all_gather(gathered, "tz", axis=0)
    gathered = lax.all_gather(gathered, "tc", axis=0)
    wv = weight_v.reshape(N_Z, N_Y, N_C, col_width, weight_v.shape[1])
    values = jnp.einsum(
        "czytf,zycfh->th", gathered, wv, preferred_element_type=jnp.float32
    ).astype(jnp.bfloat16)

    heads_here = weight_v.shape[1] // HEAD_SIZE
    query_rows = queries[0].reshape(length // LEN, LEN, heads_here, HEAD_SIZE)
    key_rows = keys[0].reshape(length // LEN, LEN, heads_here, HEAD_SIZE)
    value_rows = values.reshape(length // LEN, LEN, heads_here, HEAD_SIZE)
    scores = jnp.einsum(
        "bqhd,bkhd->bhqk", query_rows, key_rows, preferred_element_type=jnp.float32
    ) / jnp.sqrt(jnp.float32(HEAD_SIZE))
    rows = lax.broadcasted_iota(jnp.int32, (LEN, LEN), 0)
    cols = lax.broadcasted_iota(jnp.int32, (LEN, LEN), 1)
    scores = jnp.where((cols <= rows)[None, None], scores, jnp.float32(-1e30))
    top = jnp.max(scores, axis=-1, keepdims=True)
    expo = jnp.exp(scores - top)
    probs = (expo / jnp.sum(expo, axis=-1, keepdims=True)).astype(jnp.bfloat16)
    context = jnp.einsum(
        "bhqk,bkhd->bqhd", probs, value_rows, preferred_element_type=jnp.float32
    ).astype(jnp.bfloat16)
    context = context.reshape(length, heads_here * HEAD_SIZE)

    core = lax.axis_index("tc").astype(jnp.int32).reshape(1)
    mine, sib = out_proj(core, context, weight_o, col_width)
    part = mine.astype(jnp.float32) + swap(sib, "tc").astype(jnp.float32)
    part = part.astype(jnp.bfloat16).reshape(N_Z, N_Y, length, col_width)
    part = lax.psum_scatter(part, "tz", scatter_dimension=0, tiled=False)
    y_index = lax.axis_index("ty")
    keep = lax.dynamic_index_in_dim(part, y_index, 0, keepdims=False)
    send = lax.dynamic_index_in_dim(part, 1 - y_index, 0, keepdims=False)
    result = keep.astype(jnp.float32) + swap(send, "ty").astype(jnp.float32)
    result = (result + activ.astype(jnp.float32)).astype(jnp.bfloat16)
    passed = swap(result, "section")
    return passed[None]


def solution(mesh):
    n_sec, n_dp, n_t = mesh.devices.shape
    sub = Mesh(
        mesh.devices.reshape(n_sec, n_dp, N_Z, N_Y, N_C),
        ("section", "dp", "tz", "ty", "tc"),
    )
    spec = P("section", "dp", ("tz", "ty", "tc"))
    return jax.shard_map(
        on_device,
        mesh=sub,
        in_specs=(
            spec,
            spec,
            spec,
            P("section", None, ("tz", "ty", "tc")),
            P("section", ("tz", "ty", "tc"), None),
        ),
        out_specs=spec,
        check_vma=False,
    )
```

```python
import jax
import jax.numpy as jnp
from jax import lax
from jax.experimental import pallas as pl
from jax.experimental.pallas import tpu as pltpu
from jax.sharding import Mesh
from jax.sharding import PartitionSpec as P

HEAD_SIZE = 128
LEN = 256
N_Z, N_Y, N_C = 8, 2, 2
GROUPS_PER_STEP = 4


def swap(value, axis):
    return lax.ppermute(value, axis, [(0, 1), (1, 0)])


def out_proj_kernel(core_ref, ctx_ref, w_ref, mine_ref, sib_ref):
    width = mine_ref.shape[2]
    is_zero = core_ref[0] == 0
    ctx = ctx_ref[...]
    for i in range(mine_ref.shape[0]):
        lo = i * 2 * width
        d0 = jnp.dot(ctx, w_ref[:, lo:lo + width], preferred_element_type=jnp.float32)
        d1 = jnp.dot(ctx, w_ref[:, lo + width:lo + 2 * width], preferred_element_type=jnp.float32)
        d0 = d0.astype(jnp.bfloat16)
        d1 = d1.astype(jnp.bfloat16)
        mine_ref[i] = jnp.where(is_zero, d0, d1)
        sib_ref[i] = jnp.where(is_zero, d1, d0)


def out_proj(core, context, weight_o, width):
    tokens, inner = context.shape
    n_groups = weight_o.shape[1] // (N_C * width)
    step = GROUPS_PER_STEP
    out = jax.ShapeDtypeStruct((n_groups, tokens, width), jnp.bfloat16)
    return pl.pallas_call(
        out_proj_kernel,
        out_shape=(out, out),
        grid_spec=pltpu.PrefetchScalarGridSpec(
            num_scalar_prefetch=1,
            grid=(n_groups // step,),
            in_specs=[
                pl.BlockSpec((tokens, inner), lambda i, c: (0, 0)),
                pl.BlockSpec((inner, step * N_C * width), lambda i, c: (0, i)),
            ],
            out_specs=[
                pl.BlockSpec((step, tokens, width), lambda i, c: (i, 0, 0)),
                pl.BlockSpec((step, tokens, width), lambda i, c: (i, 0, 0)),
            ],
        ),
    )(core, context, weight_o)


def value_proj_kernel(core_ref, f_ref, *refs):
    w_refs, o_ref = refs[:-1], refs[-1]

    @pl.when(pl.program_id(0) == 0)
    def _():
        o_ref[...] = jnp.zeros(o_ref.shape, o_ref.dtype)

    acc = o_ref[...]
    for k, w_ref in enumerate(w_refs):
        acc = acc + jnp.dot(f_ref[k], w_ref[...], preferred_element_type=jnp.float32)
    o_ref[...] = acc


def value_proj(core, feats, weight_v):
    n_groups, tokens, width = feats.shape
    step = GROUPS_PER_STEP
    w_specs = [
        pl.BlockSpec((width, weight_v.shape[1]), lambda i, c, k=k: (N_C * (i * step + k) + c[0], 0))
        for k in range(step)
    ]
    return pl.pallas_call(
        value_proj_kernel,
        out_shape=jax.ShapeDtypeStruct((tokens, weight_v.shape[1]), jnp.float32),
        grid_spec=pltpu.PrefetchScalarGridSpec(
            num_scalar_prefetch=1,
            grid=(n_groups // step,),
            in_specs=[pl.BlockSpec((step, tokens, width), lambda i, c: (i, 0, 0))] + w_specs,
            out_specs=pl.BlockSpec((tokens, weight_v.shape[1]), lambda i, c: (0, 0)),
        ),
    )(core, feats, *([weight_v] * step))


def on_device(inputs, queries, keys, w_value, w_out):
    activ = inputs[0]
    weight_v = w_value[0]
    weight_o = w_out[0]
    length = activ.shape[0]
    col_width = activ.shape[1]
    n_feat = weight_v.shape[0]

    y_first = lax.axis_index("ty") == 0
    other = swap(activ, "ty")
    gathered = jnp.stack([jnp.where(y_first, activ, other), jnp.where(y_first, other, activ)])
    gathered = lax.all_gather(gathered, "tz", axis=0)
    from_sib = swap(gathered, "tc").reshape(N_Z * N_Y, length, col_width)
    gathered = gathered.reshape(N_Z * N_Y, length, col_width)
    c_index = lax.axis_index("tc").astype(jnp.int32)
    values = value_proj(c_index.reshape(1), gathered, weight_v)
    values = values + value_proj((1 - c_index).reshape(1), from_sib, weight_v)
    values = values.astype(jnp.bfloat16)

    heads_here = weight_v.shape[1] // HEAD_SIZE
    query_rows = queries[0].reshape(length // LEN, LEN, heads_here, HEAD_SIZE)
    key_rows = keys[0].reshape(length // LEN, LEN, heads_here, HEAD_SIZE)
    value_rows = values.reshape(length // LEN, LEN, heads_here, HEAD_SIZE)
    scores = jnp.einsum(
        "bqhd,bkhd->bhqk", query_rows, key_rows, preferred_element_type=jnp.float32
    ) / jnp.sqrt(jnp.float32(HEAD_SIZE))
    rows = lax.broadcasted_iota(jnp.int32, (LEN, LEN), 0)
    cols = lax.broadcasted_iota(jnp.int32, (LEN, LEN), 1)
    scores = jnp.where((cols <= rows)[None, None], scores, jnp.float32(-1e30))
    top = jnp.max(scores, axis=-1, keepdims=True)
    expo = jnp.exp(scores - top)
    probs = (expo / jnp.sum(expo, axis=-1, keepdims=True)).astype(jnp.bfloat16)
    context = jnp.einsum(
        "bhqk,bkhd->bqhd", probs, value_rows, preferred_element_type=jnp.float32
    ).astype(jnp.bfloat16)
    context = context.reshape(length, heads_here * HEAD_SIZE)

    core = lax.axis_index("tc").astype(jnp.int32).reshape(1)
    mine, sib = out_proj(core, context, weight_o, col_width)
    part = mine.astype(jnp.float32) + swap(sib, "tc").astype(jnp.float32)
    part = part.astype(jnp.bfloat16).reshape(N_Z, N_Y, length, col_width)
    part = lax.psum_scatter(part, "tz", scatter_dimension=0, tiled=False)
    y_index = lax.axis_index("ty")
    keep = lax.dynamic_index_in_dim(part, y_index, 0, keepdims=False)
    send = lax.dynamic_index_in_dim(part, 1 - y_index, 0, keepdims=False)
    result = keep.astype(jnp.float32) + swap(send, "ty").astype(jnp.float32)
    result = (result + activ.astype(jnp.float32)).astype(jnp.bfloat16)
    passed = swap(result, "section")
    return passed[None]


def solution(mesh):
    n_sec, n_dp, n_t = mesh.devices.shape
    sub = Mesh(
        mesh.devices.reshape(n_sec, n_dp, N_Z, N_Y, N_C),
        ("section", "dp", "tz", "ty", "tc"),
    )
    spec = P("section", "dp", ("tz", "ty", "tc"))
    return jax.shard_map(
        on_device,
        mesh=sub,
        in_specs=(
            spec,
            spec,
            spec,
            P("section", None, ("tz", "ty", "tc")),
            P("section", ("tz", "ty", "tc"), None),
        ),
        out_specs=spec,
        check_vma=False,
    )
```

```python
import jax
import jax.numpy as jnp
from jax import lax
from jax.experimental import pallas as pl
from jax.experimental.pallas import tpu as pltpu
from jax.sharding import Mesh
from jax.sharding import PartitionSpec as P

HEAD_SIZE = 128
LEN = 256
N_Z, N_Y, N_C = 8, 2, 2
GROUPS_PER_STEP = 4


def swap(value, axis):
    return lax.ppermute(value, axis, [(0, 1), (1, 0)])


def out_proj_kernel(core_ref, ctx_ref, w_ref, mine_ref, sib_ref):
    width = mine_ref.shape[2]
    is_zero = core_ref[0] == 0
    ctx = ctx_ref[...]
    for i in range(mine_ref.shape[0]):
        lo = i * 2 * width
        d0 = jnp.dot(ctx, w_ref[:, lo:lo + width], preferred_element_type=jnp.float32)
        d1 = jnp.dot(ctx, w_ref[:, lo + width:lo + 2 * width], preferred_element_type=jnp.float32)
        d0 = d0.astype(jnp.bfloat16)
        d1 = d1.astype(jnp.bfloat16)
        mine_ref[i] = jnp.where(is_zero, d0, d1)
        sib_ref[i] = jnp.where(is_zero, d1, d0)


def out_proj(core, context, weight_o, width):
    tokens, inner = context.shape
    n_groups = weight_o.shape[1] // (N_C * width)
    step = GROUPS_PER_STEP
    out = jax.ShapeDtypeStruct((n_groups, tokens, width), jnp.bfloat16)
    return pl.pallas_call(
        out_proj_kernel,
        out_shape=(out, out),
        grid_spec=pltpu.PrefetchScalarGridSpec(
            num_scalar_prefetch=1,
            grid=(n_groups // step,),
            in_specs=[
                pl.BlockSpec((tokens, inner), lambda i, c: (0, 0)),
                pl.BlockSpec((inner, step * N_C * width), lambda i, c: (0, i)),
            ],
            out_specs=[
                pl.BlockSpec((step, tokens, width), lambda i, c: (i, 0, 0)),
                pl.BlockSpec((step, tokens, width), lambda i, c: (i, 0, 0)),
            ],
        ),
    )(core, context, weight_o)


def value_proj_kernel(core_ref, f_ref, *refs):
    w_refs, o_ref = refs[:-1], refs[-1]

    @pl.when(pl.program_id(0) == 0)
    def _():
        o_ref[...] = jnp.zeros(o_ref.shape, o_ref.dtype)

    acc = o_ref[...]
    for k, w_ref in enumerate(w_refs):
        acc = acc + jnp.dot(f_ref[k], w_ref[...], preferred_element_type=jnp.float32)
    o_ref[...] = acc


def value_proj(core, feats, weight_v):
    n_groups, tokens, width = feats.shape
    step = GROUPS_PER_STEP
    w_specs = [
        pl.BlockSpec((width, weight_v.shape[1]), lambda i, c, k=k: (N_C * (i * step + k) + c[0], 0))
        for k in range(step)
    ]
    return pl.pallas_call(
        value_proj_kernel,
        out_shape=jax.ShapeDtypeStruct((tokens, weight_v.shape[1]), jnp.float32),
        grid_spec=pltpu.PrefetchScalarGridSpec(
            num_scalar_prefetch=1,
            grid=(n_groups // step,),
            in_specs=[pl.BlockSpec((step, tokens, width), lambda i, c: (i, 0, 0))] + w_specs,
            out_specs=pl.BlockSpec((tokens, weight_v.shape[1]), lambda i, c: (0, 0)),
        ),
    )(core, feats, *([weight_v] * step))


def attend(query_rows, key_rows, value_rows, offset):
    scores = jnp.einsum(
        "qhd,khd->hqk", query_rows, key_rows, preferred_element_type=jnp.float32
    ) / jnp.sqrt(jnp.float32(HEAD_SIZE))
    shape = (query_rows.shape[0], key_rows.shape[0])
    rows = lax.broadcasted_iota(jnp.int32, shape, 0) + offset
    cols = lax.broadcasted_iota(jnp.int32, shape, 1)
    scores = jnp.where((cols <= rows)[None], scores, jnp.float32(-1e30))
    top = jnp.max(scores, axis=-1, keepdims=True)
    expo = jnp.exp(scores - top)
    probs = (expo / jnp.sum(expo, axis=-1, keepdims=True)).astype(jnp.bfloat16)
    context = jnp.einsum("hqk,khd->qhd", probs, value_rows, preferred_element_type=jnp.float32)
    return context.astype(jnp.bfloat16).reshape(query_rows.shape[0], -1)


def on_device(inputs, queries, keys, w_value, w_out):
    activ = inputs[0]
    weight_v = w_value[0]
    weight_o = w_out[0]
    length = activ.shape[0]
    col_width = activ.shape[1]
    heads_here = weight_v.shape[1] // HEAD_SIZE
    half = LEN // 2
    c_index = lax.axis_index("tc").astype(jnp.int32)
    y_index = lax.axis_index("ty")

    y_first = y_index == 0
    other = swap(activ, "ty")
    gathered = jnp.stack([jnp.where(y_first, activ, other), jnp.where(y_first, other, activ)])
    query_rows = queries[0].reshape(length, heads_here, HEAD_SIZE)
    key_rows = keys[0].reshape(length, heads_here, HEAD_SIZE)

    def finish(part, lo):
        part = lax.psum_scatter(part, "tz", scatter_dimension=0, tiled=False)
        keep = lax.dynamic_index_in_dim(part, y_index, 0, keepdims=False)
        send = lax.dynamic_index_in_dim(part, 1 - y_index, 0, keepdims=False)
        result = keep.astype(jnp.float32) + swap(send, "ty").astype(jnp.float32)
        result = (result + activ[lo:lo + half].astype(jnp.float32)).astype(jnp.bfloat16)
        return swap(result, "section")

    value_parts = []
    results = []
    pending = None
    for lo in range(0, length, half):
        feats = lax.all_gather(gathered[:, lo:lo + half], "tz", axis=0)
        if pending is not None:
            feats, part = lax.optimization_barrier((feats, pending[0]))
            results.append(finish(part, pending[1]))
        from_sib = swap(feats, "tc").reshape(N_Z * N_Y, half, col_width)
        feats = feats.reshape(N_Z * N_Y, half, col_width)
        values = value_proj(c_index.reshape(1), feats, weight_v)
        values = values + value_proj((1 - c_index).reshape(1), from_sib, weight_v)
        value_parts.append(values.astype(jnp.bfloat16).reshape(half, heads_here, HEAD_SIZE))
        seen = lo + half
        value_rows = jnp.concatenate(value_parts, axis=0) if len(value_parts) > 1 else value_parts[0]
        context = attend(query_rows[lo:seen], key_rows[:seen], value_rows, lo)

        mine, sib = out_proj(c_index.reshape(1), context, weight_o, col_width)
        part = mine.astype(jnp.float32) + swap(sib, "tc").astype(jnp.float32)
        pending = (part.astype(jnp.bfloat16).reshape(N_Z, N_Y, half, col_width), lo)
    results.append(finish(*pending))
    return jnp.concatenate(results, axis=0)[None]


def solution(mesh):
    n_sec, n_dp, n_t = mesh.devices.shape
    sub = Mesh(
        mesh.devices.reshape(n_sec, n_dp, N_Z, N_Y, N_C),
        ("section", "dp", "tz", "ty", "tc"),
    )
    spec = P("section", "dp", ("tz", "ty", "tc"))
    return jax.shard_map(
        on_device,
        mesh=sub,
        in_specs=(
            spec,
            spec,
            spec,
            P("section", None, ("tz", "ty", "tc")),
            P("section", ("tz", "ty", "tc"), None),
        ),
        out_specs=spec,
        check_vma=False,
    )
```

```python
import jax
import jax.numpy as jnp
from jax import lax
from jax.experimental import pallas as pl
from jax.experimental.pallas import tpu as pltpu
from jax.sharding import Mesh
from jax.sharding import PartitionSpec as P

HEAD_SIZE = 128
LEN = 256
N_Z, N_Y, N_C = 8, 2, 2
GROUPS_PER_STEP = 4


def swap(value, axis):
    return lax.ppermute(value, axis, [(0, 1), (1, 0)])


def out_proj_kernel(core_ref, ctx_ref, w_ref, mine_ref, sib_ref):
    width = mine_ref.shape[2]
    is_zero = core_ref[0] == 0
    ctx = ctx_ref[...]
    for i in range(mine_ref.shape[0]):
        lo = i * 2 * width
        d0 = jnp.dot(ctx, w_ref[:, lo:lo + width], preferred_element_type=jnp.float32)
        d1 = jnp.dot(ctx, w_ref[:, lo + width:lo + 2 * width], preferred_element_type=jnp.float32)
        d0 = d0.astype(jnp.bfloat16)
        d1 = d1.astype(jnp.bfloat16)
        mine_ref[i] = jnp.where(is_zero, d0, d1)
        sib_ref[i] = jnp.where(is_zero, d1, d0)


def out_proj(core, context, weight_o, width):
    tokens, inner = context.shape
    n_groups = weight_o.shape[1] // (N_C * width)
    step = GROUPS_PER_STEP
    out = jax.ShapeDtypeStruct((n_groups, tokens, width), jnp.bfloat16)
    return pl.pallas_call(
        out_proj_kernel,
        out_shape=(out, out),
        grid_spec=pltpu.PrefetchScalarGridSpec(
            num_scalar_prefetch=1,
            grid=(n_groups // step,),
            in_specs=[
                pl.BlockSpec((tokens, inner), lambda i, c: (0, 0)),
                pl.BlockSpec((inner, step * N_C * width), lambda i, c: (0, i)),
            ],
            out_specs=[
                pl.BlockSpec((step, tokens, width), lambda i, c: (i, 0, 0)),
                pl.BlockSpec((step, tokens, width), lambda i, c: (i, 0, 0)),
            ],
        ),
    )(core, context, weight_o)


def value_proj_kernel(core_ref, f_ref, *refs):
    w_refs, o_ref = refs[:-1], refs[-1]

    @pl.when(pl.program_id(0) == 0)
    def _():
        o_ref[...] = jnp.zeros(o_ref.shape, o_ref.dtype)

    acc = o_ref[...]
    for k, w_ref in enumerate(w_refs):
        acc = acc + jnp.dot(f_ref[k], w_ref[...], preferred_element_type=jnp.float32)
    o_ref[...] = acc


def value_proj(core, feats, weight_v):
    n_groups, tokens, width = feats.shape
    step = GROUPS_PER_STEP
    w_specs = [
        pl.BlockSpec((width, weight_v.shape[1]), lambda i, c, k=k: (N_C * (i * step + k) + c[0], 0))
        for k in range(step)
    ]
    return pl.pallas_call(
        value_proj_kernel,
        out_shape=jax.ShapeDtypeStruct((tokens, weight_v.shape[1]), jnp.float32),
        grid_spec=pltpu.PrefetchScalarGridSpec(
            num_scalar_prefetch=1,
            grid=(n_groups // step,),
            in_specs=[pl.BlockSpec((step, tokens, width), lambda i, c: (i, 0, 0))] + w_specs,
            out_specs=pl.BlockSpec((tokens, weight_v.shape[1]), lambda i, c: (0, 0)),
        ),
    )(core, feats, *([weight_v] * step))


def on_device(inputs, queries, keys, w_value, w_out):
    activ = inputs[0]
    weight_v = w_value[0]
    weight_o = w_out[0]
    length = activ.shape[0]
    col_width = activ.shape[1]
    n_feat = weight_v.shape[0]

    y_first = lax.axis_index("ty") == 0
    other = swap(activ, "ty")
    gathered = jnp.stack([jnp.where(y_first, activ, other), jnp.where(y_first, other, activ)])
    gathered = lax.all_gather(gathered, "tz", axis=0)
    from_sib = swap(gathered, "tc").reshape(N_Z * N_Y, length, col_width)
    gathered = gathered.reshape(N_Z * N_Y, length, col_width)
    c_index = lax.axis_index("tc").astype(jnp.int32)
    values = value_proj(c_index.reshape(1), gathered, weight_v)
    values = values + value_proj((1 - c_index).reshape(1), from_sib, weight_v)
    values = values.astype(jnp.bfloat16)

    heads_here = weight_v.shape[1] // HEAD_SIZE
    query_rows = queries[0].reshape(length // LEN, LEN, heads_here, HEAD_SIZE)
    key_rows = keys[0].reshape(length // LEN, LEN, heads_here, HEAD_SIZE)
    value_rows = values.reshape(length // LEN, LEN, heads_here, HEAD_SIZE)
    scores = jnp.einsum(
        "bqhd,bkhd->bhqk", query_rows, key_rows, preferred_element_type=jnp.float32
    ) / jnp.sqrt(jnp.float32(HEAD_SIZE))
    rows = lax.broadcasted_iota(jnp.int32, (LEN, LEN), 0)
    cols = lax.broadcasted_iota(jnp.int32, (LEN, LEN), 1)
    scores = jnp.where((cols <= rows)[None, None], scores, jnp.float32(-1e30))
    top = jnp.max(scores, axis=-1, keepdims=True)
    expo = jnp.exp(scores - top)
    probs = (expo / jnp.sum(expo, axis=-1, keepdims=True)).astype(jnp.bfloat16)
    context = jnp.einsum(
        "bhqk,bkhd->bqhd", probs, value_rows, preferred_element_type=jnp.float32
    ).astype(jnp.bfloat16)
    context = context.reshape(length, heads_here * HEAD_SIZE)

    core = lax.axis_index("tc").astype(jnp.int32).reshape(1)
    mine, sib = out_proj(core, context, weight_o, col_width)
    part = mine.astype(jnp.float32) + swap(sib, "tc").astype(jnp.float32)
    part = part.astype(jnp.bfloat16).reshape(N_Z, N_Y, length, col_width)
    part = lax.psum_scatter(part, "tz", scatter_dimension=0, tiled=False)
    y_index = lax.axis_index("ty")
    keep = lax.dynamic_index_in_dim(part, y_index, 0, keepdims=False)
    send = lax.dynamic_index_in_dim(part, 1 - y_index, 0, keepdims=False)
    keep = (keep.astype(jnp.float32) + activ.astype(jnp.float32)).astype(jnp.bfloat16)
    across = lax.ppermute(send, ("section", "ty"), [(i, 3 - i) for i in range(4)])
    result = swap(keep, "section").astype(jnp.float32) + across.astype(jnp.float32)
    return result.astype(jnp.bfloat16)[None]


def solution(mesh):
    n_sec, n_dp, n_t = mesh.devices.shape
    sub = Mesh(
        mesh.devices.reshape(n_sec, n_dp, N_Z, N_Y, N_C),
        ("section", "dp", "tz", "ty", "tc"),
    )
    spec = P("section", "dp", ("tz", "ty", "tc"))
    return jax.shard_map(
        on_device,
        mesh=sub,
        in_specs=(
            spec,
            spec,
            spec,
            P("section", None, ("tz", "ty", "tc")),
            P("section", ("tz", "ty", "tc"), None),
        ),
        out_specs=spec,
        check_vma=False,
    )
```

```python
import jax
import jax.numpy as jnp
from jax import lax
from jax.experimental import pallas as pl
from jax.experimental.pallas import tpu as pltpu
from jax.sharding import Mesh
from jax.sharding import PartitionSpec as P

HEAD_SIZE = 128
LEN = 256
N_Z, N_Y, N_C = 8, 2, 2
GROUPS_PER_STEP = 4


def swap(value, axis):
    return lax.ppermute(value, axis, [(0, 1), (1, 0)])


def out_proj_kernel(core_ref, ctx_ref, w_ref, mine_ref, sib_ref):
    width = mine_ref.shape[2]
    is_zero = core_ref[0] == 0
    ctx = ctx_ref[...]
    for i in range(mine_ref.shape[0]):
        lo = i * 2 * width
        d0 = jnp.dot(ctx, w_ref[:, lo:lo + width], preferred_element_type=jnp.float32)
        d1 = jnp.dot(ctx, w_ref[:, lo + width:lo + 2 * width], preferred_element_type=jnp.float32)
        d0 = d0.astype(jnp.bfloat16)
        d1 = d1.astype(jnp.bfloat16)
        mine_ref[i] = jnp.where(is_zero, d0, d1)
        sib_ref[i] = jnp.where(is_zero, d1, d0)


def out_proj(core, context, weight_o, width):
    tokens, inner = context.shape
    n_groups = weight_o.shape[1] // (N_C * width)
    step = GROUPS_PER_STEP
    out = jax.ShapeDtypeStruct((n_groups, tokens, width), jnp.bfloat16)
    return pl.pallas_call(
        out_proj_kernel,
        out_shape=(out, out),
        grid_spec=pltpu.PrefetchScalarGridSpec(
            num_scalar_prefetch=1,
            grid=(n_groups // step,),
            in_specs=[
                pl.BlockSpec((tokens, inner), lambda i, c: (0, 0)),
                pl.BlockSpec((inner, step * N_C * width), lambda i, c: (0, i)),
            ],
            out_specs=[
                pl.BlockSpec((step, tokens, width), lambda i, c: (i, 0, 0)),
                pl.BlockSpec((step, tokens, width), lambda i, c: (i, 0, 0)),
            ],
        ),
    )(core, context, weight_o)


def gathered_proj_kernel(f_ref, *refs):
    w_refs, o_ref = refs[:-1], refs[-1]

    @pl.when(pl.program_id(0) == 0)
    def _():
        o_ref[...] = jnp.zeros(o_ref.shape, o_ref.dtype)

    acc = o_ref[...]
    for k, w_ref in enumerate(w_refs):
        acc = acc + jnp.dot(f_ref[k], w_ref[...], preferred_element_type=jnp.float32)
    o_ref[...] = acc


def gathered_proj(feats, weight_v):
    tokens, width = feats.shape[-2:]
    feats = feats.reshape(-1, tokens, width)
    step = N_C * N_Y
    w_specs = [
        pl.BlockSpec((width, weight_v.shape[1]), lambda i, c=c, y=y: (i * step + y * N_C + c, 0))
        for c in range(N_C)
        for y in range(N_Y)
    ]
    return pl.pallas_call(
        gathered_proj_kernel,
        out_shape=jax.ShapeDtypeStruct((tokens, weight_v.shape[1]), jnp.float32),
        grid=(N_Z,),
        in_specs=[pl.BlockSpec((step, tokens, width), lambda i: (i, 0, 0))] + w_specs,
        out_specs=pl.BlockSpec((tokens, weight_v.shape[1]), lambda i: (0, 0)),
    )(feats, *([weight_v] * step))


def on_device(inputs, queries, keys, w_value, w_out):
    activ = inputs[0]
    weight_v = w_value[0]
    weight_o = w_out[0]
    length = activ.shape[0]
    col_width = activ.shape[1]
    n_feat = weight_v.shape[0]

    y_first = lax.axis_index("ty") == 0
    other = swap(activ, "ty")
    gathered = jnp.stack([jnp.where(y_first, activ, other), jnp.where(y_first, other, activ)])
    gathered = lax.all_gather(gathered, ("tz", "tc"), axis=0)
    values = gathered_proj(gathered, weight_v)
    values = values.astype(jnp.bfloat16)

    heads_here = weight_v.shape[1] // HEAD_SIZE
    query_rows = queries[0].reshape(length // LEN, LEN, heads_here, HEAD_SIZE)
    key_rows = keys[0].reshape(length // LEN, LEN, heads_here, HEAD_SIZE)
    value_rows = values.reshape(length // LEN, LEN, heads_here, HEAD_SIZE)
    scores = jnp.einsum(
        "bqhd,bkhd->bhqk", query_rows, key_rows, preferred_element_type=jnp.float32
    ) / jnp.sqrt(jnp.float32(HEAD_SIZE))
    rows = lax.broadcasted_iota(jnp.int32, (LEN, LEN), 0)
    cols = lax.broadcasted_iota(jnp.int32, (LEN, LEN), 1)
    scores = jnp.where((cols <= rows)[None, None], scores, jnp.float32(-1e30))
    top = jnp.max(scores, axis=-1, keepdims=True)
    expo = jnp.exp(scores - top)
    probs = (expo / jnp.sum(expo, axis=-1, keepdims=True)).astype(jnp.bfloat16)
    context = jnp.einsum(
        "bhqk,bkhd->bqhd", probs, value_rows, preferred_element_type=jnp.float32
    ).astype(jnp.bfloat16)
    context = context.reshape(length, heads_here * HEAD_SIZE)

    core = lax.axis_index("tc").astype(jnp.int32).reshape(1)
    mine, sib = out_proj(core, context, weight_o, col_width)
    part = mine.astype(jnp.float32) + swap(sib, "tc").astype(jnp.float32)
    part = part.astype(jnp.bfloat16).reshape(N_Z, N_Y, length, col_width)
    part = lax.psum_scatter(part, "tz", scatter_dimension=0, tiled=False)
    y_index = lax.axis_index("ty")
    keep = lax.dynamic_index_in_dim(part, y_index, 0, keepdims=False)
    send = lax.dynamic_index_in_dim(part, 1 - y_index, 0, keepdims=False)
    keep = (keep.astype(jnp.float32) + activ.astype(jnp.float32)).astype(jnp.bfloat16)
    across = lax.ppermute(send, ("section", "ty"), [(i, 3 - i) for i in range(4)])
    result = swap(keep, "section").astype(jnp.float32) + across.astype(jnp.float32)
    return result.astype(jnp.bfloat16)[None]


def solution(mesh):
    n_sec, n_dp, n_t = mesh.devices.shape
    sub = Mesh(
        mesh.devices.reshape(n_sec, n_dp, N_Z, N_Y, N_C),
        ("section", "dp", "tz", "ty", "tc"),
    )
    spec = P("section", "dp", ("tz", "ty", "tc"))
    return jax.shard_map(
        on_device,
        mesh=sub,
        in_specs=(
            spec,
            spec,
            spec,
            P("section", None, ("tz", "ty", "tc")),
            P("section", ("tz", "ty", "tc"), None),
        ),
        out_specs=spec,
        check_vma=False,
    )
```

```python
import jax
import jax.numpy as jnp
from jax import lax
from jax.experimental import pallas as pl
from jax.experimental.pallas import tpu as pltpu
from jax.sharding import Mesh
from jax.sharding import PartitionSpec as P

HEAD_SIZE = 128
LEN = 256
N_Z, N_Y, N_C = 8, 2, 2
GROUPS_PER_STEP = 4
Z_PER_STEP = 2


def swap(value, axis):
    return lax.ppermute(value, axis, [(0, 1), (1, 0)])


def out_proj_kernel(core_ref, ctx_ref, *refs):
    w_refs, o_ref = refs[:-1], refs[-1]
    ctx = ctx_ref[...]
    for k, w_ref in enumerate(w_refs):
        d = jnp.dot(ctx, w_ref[...], preferred_element_type=jnp.float32)
        o_ref[k] = d.astype(jnp.bfloat16)


def out_proj(core, context, weight_o, width):
    tokens, inner = context.shape
    n_groups = weight_o.shape[1] // (N_C * width)
    step = GROUPS_PER_STEP
    w_specs = [
        pl.BlockSpec((inner, width), lambda i, c, k=k: (0, N_C * (i * step + k) + c[0]))
        for k in range(step)
    ]
    return pl.pallas_call(
        out_proj_kernel,
        out_shape=jax.ShapeDtypeStruct((n_groups, tokens, width), jnp.bfloat16),
        grid_spec=pltpu.PrefetchScalarGridSpec(
            num_scalar_prefetch=1,
            grid=(n_groups // step,),
            in_specs=[pl.BlockSpec((tokens, inner), lambda i, c: (0, 0))] + w_specs,
            out_specs=pl.BlockSpec((step, tokens, width), lambda i, c: (i, 0, 0)),
        ),
    )(core, context, *([weight_o] * step))


def gathered_proj_kernel(f_ref, *refs):
    w_refs, o_ref = refs[:-1], refs[-1]

    @pl.when(pl.program_id(0) == 0)
    def _():
        o_ref[...] = jnp.zeros(o_ref.shape, o_ref.dtype)

    acc = o_ref[...]
    for k, w_ref in enumerate(w_refs):
        acc = acc + jnp.dot(f_ref[k], w_ref[...], preferred_element_type=jnp.float32)
    o_ref[...] = acc


def gathered_proj(feats, weight_v):
    tokens, width = feats.shape[-2:]
    feats = feats.reshape(-1, tokens, width)
    per_z = N_C * N_Y
    step = Z_PER_STEP * per_z
    w_specs = [
        pl.BlockSpec(
            (width, weight_v.shape[1]),
            lambda i, z=z, c=c, y=y: ((i * Z_PER_STEP + z) * per_z + y * N_C + c, 0),
        )
        for z in range(Z_PER_STEP)
        for c in range(N_C)
        for y in range(N_Y)
    ]
    return pl.pallas_call(
        gathered_proj_kernel,
        out_shape=jax.ShapeDtypeStruct((tokens, weight_v.shape[1]), jnp.float32),
        grid=(N_Z // Z_PER_STEP,),
        in_specs=[pl.BlockSpec((step, tokens, width), lambda i: (i, 0, 0))] + w_specs,
        out_specs=pl.BlockSpec((tokens, weight_v.shape[1]), lambda i: (0, 0)),
    )(feats, *([weight_v] * step))


def on_device(inputs, queries, keys, w_value, w_out):
    activ = inputs[0]
    weight_v = w_value[0]
    weight_o = w_out[0]
    length = activ.shape[0]
    col_width = activ.shape[1]
    n_feat = weight_v.shape[0]

    y_first = lax.axis_index("ty") == 0
    other = swap(activ, "ty")
    gathered = jnp.stack([jnp.where(y_first, activ, other), jnp.where(y_first, other, activ)])
    gathered = lax.all_gather(gathered, ("tz", "tc"), axis=0)
    values = gathered_proj(gathered, weight_v)
    values = values.astype(jnp.bfloat16)

    heads_here = weight_v.shape[1] // HEAD_SIZE
    query_rows = queries[0].reshape(length // LEN, LEN, heads_here, HEAD_SIZE)
    key_rows = keys[0].reshape(length // LEN, LEN, heads_here, HEAD_SIZE)
    value_rows = values.reshape(length // LEN, LEN, heads_here, HEAD_SIZE)
    scores = jnp.einsum(
        "bqhd,bkhd->bhqk", query_rows, key_rows, preferred_element_type=jnp.float32
    ) / jnp.sqrt(jnp.float32(HEAD_SIZE))
    rows = lax.broadcasted_iota(jnp.int32, (LEN, LEN), 0)
    cols = lax.broadcasted_iota(jnp.int32, (LEN, LEN), 1)
    scores = jnp.where((cols <= rows)[None, None], scores, jnp.float32(-1e30))
    top = jnp.max(scores, axis=-1, keepdims=True)
    expo = jnp.exp(scores - top)
    probs = (expo / jnp.sum(expo, axis=-1, keepdims=True)).astype(jnp.bfloat16)
    context = jnp.einsum(
        "bhqk,bkhd->bqhd", probs, value_rows, preferred_element_type=jnp.float32
    ).astype(jnp.bfloat16)
    context = context.reshape(length, heads_here * HEAD_SIZE)

    core = lax.axis_index("tc").astype(jnp.int32).reshape(1)
    sib = out_proj(1 - core, context, weight_o, col_width)
    from_sib = swap(sib, "tc")
    mine = out_proj(core, context, weight_o, col_width)
    part = mine.astype(jnp.float32) + from_sib.astype(jnp.float32)
    part = part.astype(jnp.bfloat16).reshape(N_Z, N_Y, length, col_width)
    part = lax.psum_scatter(part, "tz", scatter_dimension=0, tiled=False)
    y_index = lax.axis_index("ty")
    keep = lax.dynamic_index_in_dim(part, y_index, 0, keepdims=False)
    send = lax.dynamic_index_in_dim(part, 1 - y_index, 0, keepdims=False)
    keep = (keep.astype(jnp.float32) + activ.astype(jnp.float32)).astype(jnp.bfloat16)
    across = lax.ppermute(send, ("section", "ty"), [(i, 3 - i) for i in range(4)])
    result = swap(keep, "section").astype(jnp.float32) + across.astype(jnp.float32)
    return result.astype(jnp.bfloat16)[None]


def solution(mesh):
    n_sec, n_dp, n_t = mesh.devices.shape
    sub = Mesh(
        mesh.devices.reshape(n_sec, n_dp, N_Z, N_Y, N_C),
        ("section", "dp", "tz", "ty", "tc"),
    )
    spec = P("section", "dp", ("tz", "ty", "tc"))
    return jax.shard_map(
        on_device,
        mesh=sub,
        in_specs=(
            spec,
            spec,
            spec,
            P("section", None, ("tz", "ty", "tc")),
            P("section", ("tz", "ty", "tc"), None),
        ),
        out_specs=spec,
        check_vma=False,
    )
```

```python
import jax
import jax.numpy as jnp
from jax import lax
from jax.experimental import pallas as pl
from jax.experimental.pallas import tpu as pltpu
from jax.sharding import Mesh
from jax.sharding import PartitionSpec as P

HEAD_SIZE = 128
LEN = 256
N_Z, N_Y, N_C = 8, 2, 2
GROUPS_PER_STEP = 4
Z_PER_STEP = 2


def swap(value, axis):
    return lax.ppermute(value, axis, [(0, 1), (1, 0)])


def out_proj_kernel(sel_ref, ctx_ref, *refs):
    w_refs, o_ref = refs[:-1], refs[-1]
    ctx = ctx_ref[...]
    for k, w_ref in enumerate(w_refs):
        d = jnp.dot(ctx, w_ref[...], preferred_element_type=jnp.float32)
        o_ref[k] = d.astype(jnp.bfloat16)


def out_proj(sel, context, weight_o, width):
    tokens, inner = context.shape
    n_groups = weight_o.shape[1] // (N_C * width)
    step = GROUPS_PER_STEP

    def w_index(i, c, k):
        z = i * (step // N_Y) + k // N_Y
        return (0, N_C * (z * N_Y + (k % N_Y + c[1]) % N_Y) + c[0])

    w_specs = [pl.BlockSpec((inner, width), lambda i, c, k=k: w_index(i, c, k)) for k in range(step)]
    return pl.pallas_call(
        out_proj_kernel,
        out_shape=jax.ShapeDtypeStruct((n_groups, tokens, width), jnp.bfloat16),
        grid_spec=pltpu.PrefetchScalarGridSpec(
            num_scalar_prefetch=1,
            grid=(n_groups // step,),
            in_specs=[pl.BlockSpec((tokens, inner), lambda i, c: (0, 0))] + w_specs,
            out_specs=pl.BlockSpec((step, tokens, width), lambda i, c: (i, 0, 0)),
        ),
    )(sel, context, *([weight_o] * step))


def gathered_proj_kernel(y_ref, f_ref, *refs):
    w_refs, o_ref = refs[:-1], refs[-1]

    @pl.when(pl.program_id(0) == 0)
    def _():
        o_ref[...] = jnp.zeros(o_ref.shape, o_ref.dtype)

    acc = o_ref[...]
    for k, w_ref in enumerate(w_refs):
        acc = acc + jnp.dot(f_ref[k], w_ref[...], preferred_element_type=jnp.float32)
    o_ref[...] = acc


def gathered_proj(y_index, feats, weight_v):
    tokens, width = feats.shape[-2:]
    feats = feats.reshape(-1, tokens, width)
    per_z = N_C * N_Y
    step = Z_PER_STEP * per_z
    w_specs = [
        pl.BlockSpec(
            (width, weight_v.shape[1]),
            lambda i, yi, z=z, c=c, y=y: (
                (i * Z_PER_STEP + z) * per_z + ((y + yi[0]) % N_Y) * N_C + c, 0
            ),
        )
        for z in range(Z_PER_STEP)
        for c in range(N_C)
        for y in range(N_Y)
    ]
    return pl.pallas_call(
        gathered_proj_kernel,
        out_shape=jax.ShapeDtypeStruct((tokens, weight_v.shape[1]), jnp.float32),
        grid_spec=pltpu.PrefetchScalarGridSpec(
            num_scalar_prefetch=1,
            grid=(N_Z // Z_PER_STEP,),
            in_specs=[pl.BlockSpec((step, tokens, width), lambda i, yi: (i, 0, 0))] + w_specs,
            out_specs=pl.BlockSpec((tokens, weight_v.shape[1]), lambda i, yi: (0, 0)),
        ),
    )(y_index, feats, *([weight_v] * step))


def on_device(inputs, queries, keys, w_value, w_out):
    activ = inputs[0]
    weight_v = w_value[0]
    weight_o = w_out[0]
    length = activ.shape[0]
    col_width = activ.shape[1]
    n_feat = weight_v.shape[0]

    y_index = lax.axis_index("ty").astype(jnp.int32)
    gathered = jnp.stack([activ, swap(activ, "ty")])
    gathered = lax.all_gather(gathered, ("tz", "tc"), axis=0)
    values = gathered_proj(y_index.reshape(1), gathered, weight_v)
    values = values.astype(jnp.bfloat16)

    heads_here = weight_v.shape[1] // HEAD_SIZE
    query_rows = queries[0].reshape(length // LEN, LEN, heads_here, HEAD_SIZE)
    key_rows = keys[0].reshape(length // LEN, LEN, heads_here, HEAD_SIZE)
    value_rows = values.reshape(length // LEN, LEN, heads_here, HEAD_SIZE)
    scores = jnp.einsum(
        "bqhd,bkhd->bhqk", query_rows, key_rows, preferred_element_type=jnp.float32
    ) / jnp.sqrt(jnp.float32(HEAD_SIZE))
    rows = lax.broadcasted_iota(jnp.int32, (LEN, LEN), 0)
    cols = lax.broadcasted_iota(jnp.int32, (LEN, LEN), 1)
    scores = jnp.where((cols <= rows)[None, None], scores, jnp.float32(-1e30))
    top = jnp.max(scores, axis=-1, keepdims=True)
    expo = jnp.exp(scores - top)
    probs = (expo / jnp.sum(expo, axis=-1, keepdims=True)).astype(jnp.bfloat16)
    context = jnp.einsum(
        "bhqk,bkhd->bqhd", probs, value_rows, preferred_element_type=jnp.float32
    ).astype(jnp.bfloat16)
    context = context.reshape(length, heads_here * HEAD_SIZE)

    core = lax.axis_index("tc").astype(jnp.int32)
    sib = out_proj(jnp.stack([1 - core, y_index]), context, weight_o, col_width)
    from_sib = swap(sib, "tc")
    mine = out_proj(jnp.stack([core, y_index]), context, weight_o, col_width)
    part = mine.astype(jnp.float32) + from_sib.astype(jnp.float32)
    part = part.astype(jnp.bfloat16).reshape(N_Z, N_Y, length, col_width)
    part = lax.psum_scatter(part, "tz", scatter_dimension=0, tiled=False)
    keep, send = part[0], part[1]
    keep = (keep.astype(jnp.float32) + activ.astype(jnp.float32)).astype(jnp.bfloat16)
    across = lax.ppermute(send, ("section", "ty"), [(i, 3 - i) for i in range(4)])
    result = swap(keep, "section").astype(jnp.float32) + across.astype(jnp.float32)
    return result.astype(jnp.bfloat16)[None]


def solution(mesh):
    n_sec, n_dp, n_t = mesh.devices.shape
    sub = Mesh(
        mesh.devices.reshape(n_sec, n_dp, N_Z, N_Y, N_C),
        ("section", "dp", "tz", "ty", "tc"),
    )
    spec = P("section", "dp", ("tz", "ty", "tc"))
    return jax.shard_map(
        on_device,
        mesh=sub,
        in_specs=(
            spec,
            spec,
            spec,
            P("section", None, ("tz", "ty", "tc")),
            P("section", ("tz", "ty", "tc"), None),
        ),
        out_specs=spec,
        check_vma=False,
    )
```

```python
import jax
import jax.numpy as jnp
from jax import lax
from jax.experimental import pallas as pl
from jax.experimental.pallas import tpu as pltpu
from jax.sharding import Mesh
from jax.sharding import PartitionSpec as P

HEAD_SIZE = 128
LEN = 256
N_Z, N_Y, N_C = 8, 2, 2
GROUPS_PER_STEP = 4
Z_PER_STEP = 2


def swap(value, axis):
    return lax.ppermute(value, axis, [(0, 1), (1, 0)])


def column_spec(inner, width, step, k):
    return pl.BlockSpec((inner, width), lambda i, c: (0, N_C * (i * step + k) + c[0]))


def pick_kernel(sel_ref, *refs):
    w_refs, o_ref = refs[:-1], refs[-1]
    for k, w_ref in enumerate(w_refs):
        o_ref[k] = w_ref[...]


def pick_columns(sel, weight_o, width):
    inner = weight_o.shape[0]
    n_groups = weight_o.shape[1] // (N_C * width)
    step = GROUPS_PER_STEP
    return pl.pallas_call(
        pick_kernel,
        out_shape=jax.ShapeDtypeStruct((n_groups, inner, width), weight_o.dtype),
        grid_spec=pltpu.PrefetchScalarGridSpec(
            num_scalar_prefetch=1,
            grid=(n_groups // step,),
            in_specs=[column_spec(inner, width, step, k) for k in range(step)],
            out_specs=pl.BlockSpec((step, inner, width), lambda i, c: (i, 0, 0)),
        ),
    )(sel, *([weight_o] * step))


def out_proj_kernel(core_ref, ctx_ref, ctx_sib_ref, w_sib_ref, *refs):
    w_refs, o_ref = refs[:-1], refs[-1]
    ctx = ctx_ref[...]
    ctx_sib = ctx_sib_ref[...]
    for k, w_ref in enumerate(w_refs):
        d = jnp.dot(ctx, w_ref[...], preferred_element_type=jnp.float32)
        d = d + jnp.dot(ctx_sib, w_sib_ref[k], preferred_element_type=jnp.float32)
        o_ref[k] = d.astype(jnp.bfloat16)


def out_proj(core, context, context_sib, weight_sib, weight_o, width):
    tokens, inner = context.shape
    n_groups = weight_o.shape[1] // (N_C * width)
    step = GROUPS_PER_STEP
    return pl.pallas_call(
        out_proj_kernel,
        out_shape=jax.ShapeDtypeStruct((n_groups, tokens, width), jnp.bfloat16),
        grid_spec=pltpu.PrefetchScalarGridSpec(
            num_scalar_prefetch=1,
            grid=(n_groups // step,),
            in_specs=[
                pl.BlockSpec((tokens, inner), lambda i, c: (0, 0)),
                pl.BlockSpec((tokens, inner), lambda i, c: (0, 0)),
                pl.BlockSpec((step, inner, width), lambda i, c: (i, 0, 0)),
            ]
            + [column_spec(inner, width, step, k) for k in range(step)],
            out_specs=pl.BlockSpec((step, tokens, width), lambda i, c: (i, 0, 0)),
        ),
    )(core, context, context_sib, weight_sib, *([weight_o] * step))


def gathered_proj_kernel(f_ref, *refs):
    w_refs, o_ref = refs[:-1], refs[-1]

    @pl.when(pl.program_id(0) == 0)
    def _():
        o_ref[...] = jnp.zeros(o_ref.shape, o_ref.dtype)

    acc = o_ref[...]
    for k, w_ref in enumerate(w_refs):
        acc = acc + jnp.dot(f_ref[k], w_ref[...], preferred_element_type=jnp.float32)
    o_ref[...] = acc


def gathered_proj(feats, weight_v):
    tokens, width = feats.shape[-2:]
    feats = feats.reshape(-1, tokens, width)
    per_z = N_C * N_Y
    step = Z_PER_STEP * per_z
    w_specs = [
        pl.BlockSpec(
            (width, weight_v.shape[1]),
            lambda i, z=z, c=c, y=y: ((i * Z_PER_STEP + z) * per_z + y * N_C + c, 0),
        )
        for z in range(Z_PER_STEP)
        for c in range(N_C)
        for y in range(N_Y)
    ]
    return pl.pallas_call(
        gathered_proj_kernel,
        out_shape=jax.ShapeDtypeStruct((tokens, weight_v.shape[1]), jnp.float32),
        grid=(N_Z // Z_PER_STEP,),
        in_specs=[pl.BlockSpec((step, tokens, width), lambda i: (i, 0, 0))] + w_specs,
        out_specs=pl.BlockSpec((tokens, weight_v.shape[1]), lambda i: (0, 0)),
    )(feats, *([weight_v] * step))


def on_device(inputs, queries, keys, w_value, w_out):
    activ = inputs[0]
    weight_v = w_value[0]
    weight_o = w_out[0]
    length = activ.shape[0]
    col_width = activ.shape[1]
    n_feat = weight_v.shape[0]

    core = lax.axis_index("tc").astype(jnp.int32).reshape(1)
    weight_from_sib = swap(pick_columns(1 - core, weight_o, col_width), "tc")
    y_first = lax.axis_index("ty") == 0
    other = swap(activ, "ty")
    gathered = jnp.stack([jnp.where(y_first, activ, other), jnp.where(y_first, other, activ)])
    gathered = lax.all_gather(gathered, ("tz", "tc"), axis=0)
    values = gathered_proj(gathered, weight_v)
    values = values.astype(jnp.bfloat16)

    heads_here = weight_v.shape[1] // HEAD_SIZE
    query_rows = queries[0].reshape(length // LEN, LEN, heads_here, HEAD_SIZE)
    key_rows = keys[0].reshape(length // LEN, LEN, heads_here, HEAD_SIZE)
    value_rows = values.reshape(length // LEN, LEN, heads_here, HEAD_SIZE)
    scores = jnp.einsum(
        "bqhd,bkhd->bhqk", query_rows, key_rows, preferred_element_type=jnp.float32
    ) / jnp.sqrt(jnp.float32(HEAD_SIZE))
    rows = lax.broadcasted_iota(jnp.int32, (LEN, LEN), 0)
    cols = lax.broadcasted_iota(jnp.int32, (LEN, LEN), 1)
    scores = jnp.where((cols <= rows)[None, None], scores, jnp.float32(-1e30))
    top = jnp.max(scores, axis=-1, keepdims=True)
    expo = jnp.exp(scores - top)
    probs = (expo / jnp.sum(expo, axis=-1, keepdims=True)).astype(jnp.bfloat16)
    context = jnp.einsum(
        "bhqk,bkhd->bqhd", probs, value_rows, preferred_element_type=jnp.float32
    ).astype(jnp.bfloat16)
    context = context.reshape(length, heads_here * HEAD_SIZE)

    part = out_proj(core, context, swap(context, "tc"), weight_from_sib, weight_o, col_width)
    part = part.reshape(N_Z, N_Y, length, col_width)
    part = lax.psum_scatter(part, "tz", scatter_dimension=0, tiled=False)
    y_index = lax.axis_index("ty")
    keep = lax.dynamic_index_in_dim(part, y_index, 0, keepdims=False)
    send = lax.dynamic_index_in_dim(part, 1 - y_index, 0, keepdims=False)
    keep = (keep.astype(jnp.float32) + activ.astype(jnp.float32)).astype(jnp.bfloat16)
    across = lax.ppermute(send, ("section", "ty"), [(i, 3 - i) for i in range(4)])
    result = swap(keep, "section").astype(jnp.float32) + across.astype(jnp.float32)
    return result.astype(jnp.bfloat16)[None]


def solution(mesh):
    n_sec, n_dp, n_t = mesh.devices.shape
    sub = Mesh(
        mesh.devices.reshape(n_sec, n_dp, N_Z, N_Y, N_C),
        ("section", "dp", "tz", "ty", "tc"),
    )
    spec = P("section", "dp", ("tz", "ty", "tc"))
    return jax.shard_map(
        on_device,
        mesh=sub,
        in_specs=(
            spec,
            spec,
            spec,
            P("section", None, ("tz", "ty", "tc")),
            P("section", ("tz", "ty", "tc"), None),
        ),
        out_specs=spec,
        check_vma=False,
    )
```

```python
import jax
import jax.numpy as jnp
from jax import lax
from jax.experimental import pallas as pl
from jax.experimental.pallas import tpu as pltpu
from jax.sharding import Mesh
from jax.sharding import PartitionSpec as P

HEAD_SIZE = 128
LEN = 256
N_Z, N_Y, N_C = 8, 2, 2
GROUPS_PER_STEP = 8
Z_PER_STEP = 4


def swap(value, axis):
    return lax.ppermute(value, axis, [(0, 1), (1, 0)])


def column_spec(inner, width, step, k):
    return pl.BlockSpec((inner, width), lambda i, c: (0, N_C * (i * step + k) + c[0]))


def pick_kernel(sel_ref, *refs):
    w_refs, o_ref = refs[:-1], refs[-1]
    for k, w_ref in enumerate(w_refs):
        o_ref[k] = w_ref[...]


def pick_columns(sel, weight_o, width):
    inner = weight_o.shape[0]
    n_groups = weight_o.shape[1] // (N_C * width)
    step = GROUPS_PER_STEP
    return pl.pallas_call(
        pick_kernel,
        out_shape=jax.ShapeDtypeStruct((n_groups, inner, width), weight_o.dtype),
        grid_spec=pltpu.PrefetchScalarGridSpec(
            num_scalar_prefetch=1,
            grid=(n_groups // step,),
            in_specs=[column_spec(inner, width, step, k) for k in range(step)],
            out_specs=pl.BlockSpec((step, inner, width), lambda i, c: (i, 0, 0)),
        ),
    )(sel, *([weight_o] * step))


def out_proj_kernel(core_ref, ctx_ref, ctx_sib_ref, w_sib_ref, *refs):
    w_refs, o_ref = refs[:-1], refs[-1]
    ctx = ctx_ref[...]
    ctx_sib = ctx_sib_ref[...]
    for k, w_ref in enumerate(w_refs):
        d = jnp.dot(ctx, w_ref[...], preferred_element_type=jnp.float32)
        d = d + jnp.dot(ctx_sib, w_sib_ref[k], preferred_element_type=jnp.float32)
        o_ref[k] = d.astype(jnp.bfloat16)


def out_proj(core, context, context_sib, weight_sib, weight_o, width):
    tokens, inner = context.shape
    n_groups = weight_o.shape[1] // (N_C * width)
    step = GROUPS_PER_STEP
    return pl.pallas_call(
        out_proj_kernel,
        out_shape=jax.ShapeDtypeStruct((n_groups, tokens, width), jnp.bfloat16),
        grid_spec=pltpu.PrefetchScalarGridSpec(
            num_scalar_prefetch=1,
            grid=(n_groups // step,),
            in_specs=[
                pl.BlockSpec((tokens, inner), lambda i, c: (0, 0)),
                pl.BlockSpec((tokens, inner), lambda i, c: (0, 0)),
                pl.BlockSpec((step, inner, width), lambda i, c: (i, 0, 0)),
            ]
            + [column_spec(inner, width, step, k) for k in range(step)],
            out_specs=pl.BlockSpec((step, tokens, width), lambda i, c: (i, 0, 0)),
        ),
    )(core, context, context_sib, weight_sib, *([weight_o] * step))


def gathered_proj_kernel(f_ref, *refs):
    w_refs, o_ref = refs[:-1], refs[-1]

    @pl.when(pl.program_id(0) == 0)
    def _():
        o_ref[...] = jnp.zeros(o_ref.shape, o_ref.dtype)

    acc = o_ref[...]
    for k, w_ref in enumerate(w_refs):
        acc = acc + jnp.dot(f_ref[k], w_ref[...], preferred_element_type=jnp.float32)
    o_ref[...] = acc


def gathered_proj(feats, weight_v):
    tokens, width = feats.shape[-2:]
    feats = feats.reshape(-1, tokens, width)
    per_z = N_C * N_Y
    step = Z_PER_STEP * per_z
    w_specs = [
        pl.BlockSpec(
            (width, weight_v.shape[1]),
            lambda i, z=z, c=c, y=y: ((i * Z_PER_STEP + z) * per_z + y * N_C + c, 0),
        )
        for z in range(Z_PER_STEP)
        for c in range(N_C)
        for y in range(N_Y)
    ]
    return pl.pallas_call(
        gathered_proj_kernel,
        out_shape=jax.ShapeDtypeStruct((tokens, weight_v.shape[1]), jnp.float32),
        grid=(N_Z // Z_PER_STEP,),
        in_specs=[pl.BlockSpec((step, tokens, width), lambda i: (i, 0, 0))] + w_specs,
        out_specs=pl.BlockSpec((tokens, weight_v.shape[1]), lambda i: (0, 0)),
    )(feats, *([weight_v] * step))


def on_device(inputs, queries, keys, w_value, w_out):
    activ = inputs[0]
    weight_v = w_value[0]
    weight_o = w_out[0]
    length = activ.shape[0]
    col_width = activ.shape[1]
    n_feat = weight_v.shape[0]

    core = lax.axis_index("tc").astype(jnp.int32).reshape(1)
    weight_from_sib = swap(pick_columns(1 - core, weight_o, col_width), "tc")
    y_first = lax.axis_index("ty") == 0
    other = swap(activ, "ty")
    gathered = jnp.stack([jnp.where(y_first, activ, other), jnp.where(y_first, other, activ)])
    gathered = lax.all_gather(gathered, ("tz", "tc"), axis=0)
    values = gathered_proj(gathered, weight_v)
    values = values.astype(jnp.bfloat16)

    heads_here = weight_v.shape[1] // HEAD_SIZE
    query_rows = queries[0].reshape(length // LEN, LEN, heads_here, HEAD_SIZE)
    key_rows = keys[0].reshape(length // LEN, LEN, heads_here, HEAD_SIZE)
    value_rows = values.reshape(length // LEN, LEN, heads_here, HEAD_SIZE)
    scores = jnp.einsum(
        "bqhd,bkhd->bhqk", query_rows, key_rows, preferred_element_type=jnp.float32
    ) / jnp.sqrt(jnp.float32(HEAD_SIZE))
    rows = lax.broadcasted_iota(jnp.int32, (LEN, LEN), 0)
    cols = lax.broadcasted_iota(jnp.int32, (LEN, LEN), 1)
    scores = jnp.where((cols <= rows)[None, None], scores, jnp.float32(-1e30))
    top = jnp.max(scores, axis=-1, keepdims=True)
    expo = jnp.exp(scores - top)
    probs = (expo / jnp.sum(expo, axis=-1, keepdims=True)).astype(jnp.bfloat16)
    context = jnp.einsum(
        "bhqk,bkhd->bqhd", probs, value_rows, preferred_element_type=jnp.float32
    ).astype(jnp.bfloat16)
    context = context.reshape(length, heads_here * HEAD_SIZE)

    part = out_proj(core, context, swap(context, "tc"), weight_from_sib, weight_o, col_width)
    part = part.reshape(N_Z, N_Y, length, col_width)
    part = lax.psum_scatter(part, "tz", scatter_dimension=0, tiled=False)
    y_index = lax.axis_index("ty")
    keep = lax.dynamic_index_in_dim(part, y_index, 0, keepdims=False)
    send = lax.dynamic_index_in_dim(part, 1 - y_index, 0, keepdims=False)
    keep = (keep.astype(jnp.float32) + activ.astype(jnp.float32)).astype(jnp.bfloat16)
    across = lax.ppermute(send, ("section", "ty"), [(i, 3 - i) for i in range(4)])
    result = swap(keep, "section").astype(jnp.float32) + across.astype(jnp.float32)
    return result.astype(jnp.bfloat16)[None]


def solution(mesh):
    n_sec, n_dp, n_t = mesh.devices.shape
    sub = Mesh(
        mesh.devices.reshape(n_sec, n_dp, N_Z, N_Y, N_C),
        ("section", "dp", "tz", "ty", "tc"),
    )
    spec = P("section", "dp", ("tz", "ty", "tc"))
    return jax.shard_map(
        on_device,
        mesh=sub,
        in_specs=(
            spec,
            spec,
            spec,
            P("section", None, ("tz", "ty", "tc")),
            P("section", ("tz", "ty", "tc"), None),
        ),
        out_specs=spec,
        check_vma=False,
    )
```

```python
import jax
import jax.numpy as jnp
from jax import lax
from jax.experimental import pallas as pl
from jax.experimental.pallas import tpu as pltpu
from jax.sharding import Mesh
from jax.sharding import PartitionSpec as P

HEAD_SIZE = 128
LEN = 256
N_Z, N_Y, N_C = 8, 2, 2
GROUPS_PER_STEP = 8
Z_PER_STEP = 4


def swap(value, axis):
    return lax.ppermute(value, axis, [(0, 1), (1, 0)])


def column_spec(inner, width, step, k):
    return pl.BlockSpec((inner, width), lambda i, c: (0, N_C * (i * step + k) + c[0]))


def pick_kernel(sel_ref, *refs):
    w_refs, o_ref = refs[:-1], refs[-1]
    for k, w_ref in enumerate(w_refs):
        o_ref[k] = w_ref[...]


def pick_columns(sel, weight_o, width):
    inner = weight_o.shape[0]
    n_groups = weight_o.shape[1] // (N_C * width)
    step = GROUPS_PER_STEP
    return pl.pallas_call(
        pick_kernel,
        out_shape=jax.ShapeDtypeStruct((n_groups, inner, width), weight_o.dtype),
        grid_spec=pltpu.PrefetchScalarGridSpec(
            num_scalar_prefetch=1,
            grid=(n_groups // step,),
            in_specs=[column_spec(inner, width, step, k) for k in range(step)],
            out_specs=pl.BlockSpec((step, inner, width), lambda i, c: (i, 0, 0)),
        ),
    )(sel, *([weight_o] * step))


def out_proj_kernel(sel_ref, ctx_ref, ctx_sib_ref, w_sib_ref, activ_ref, *refs):
    w_refs, o_ref = refs[:-1], refs[-1]
    ctx = ctx_ref[...]
    ctx_sib = ctx_sib_ref[...]
    activ = activ_ref[...].astype(jnp.float32)
    first = pl.program_id(0) * len(w_refs)
    for k, w_ref in enumerate(w_refs):
        d = jnp.dot(ctx, w_ref[...], preferred_element_type=jnp.float32)
        d = d + jnp.dot(ctx_sib, w_sib_ref[k], preferred_element_type=jnp.float32)
        d = d + jnp.where(first + k == sel_ref[1], activ, jnp.zeros_like(activ))
        o_ref[k] = d.astype(jnp.bfloat16)


def out_proj(sel, context, context_sib, weight_sib, activ, weight_o, width):
    tokens, inner = context.shape
    n_groups = weight_o.shape[1] // (N_C * width)
    step = GROUPS_PER_STEP
    return pl.pallas_call(
        out_proj_kernel,
        out_shape=jax.ShapeDtypeStruct((n_groups, tokens, width), jnp.bfloat16),
        grid_spec=pltpu.PrefetchScalarGridSpec(
            num_scalar_prefetch=1,
            grid=(n_groups // step,),
            in_specs=[
                pl.BlockSpec((tokens, inner), lambda i, c: (0, 0)),
                pl.BlockSpec((tokens, inner), lambda i, c: (0, 0)),
                pl.BlockSpec((step, inner, width), lambda i, c: (i, 0, 0)),
                pl.BlockSpec((tokens, width), lambda i, c: (0, 0)),
            ]
            + [column_spec(inner, width, step, k) for k in range(step)],
            out_specs=pl.BlockSpec((step, tokens, width), lambda i, c: (i, 0, 0)),
        ),
    )(sel, context, context_sib, weight_sib, activ, *([weight_o] * step))


def gathered_proj_kernel(f_ref, *refs):
    w_refs, o_ref, acc_ref = refs[:-2], refs[-2], refs[-1]

    @pl.when(pl.program_id(0) == 0)
    def _():
        acc_ref[...] = jnp.zeros(acc_ref.shape, acc_ref.dtype)

    acc = acc_ref[...]
    for k, w_ref in enumerate(w_refs):
        acc = acc + jnp.dot(f_ref[k], w_ref[...], preferred_element_type=jnp.float32)
    acc_ref[...] = acc

    @pl.when(pl.program_id(0) == pl.num_programs(0) - 1)
    def _():
        o_ref[...] = acc.astype(o_ref.dtype)


def gathered_proj(feats, weight_v):
    tokens, width = feats.shape[-2:]
    feats = feats.reshape(-1, tokens, width)
    per_z = N_C * N_Y
    step = Z_PER_STEP * per_z
    w_specs = [
        pl.BlockSpec(
            (width, weight_v.shape[1]),
            lambda i, z=z, c=c, y=y: ((i * Z_PER_STEP + z) * per_z + y * N_C + c, 0),
        )
        for z in range(Z_PER_STEP)
        for c in range(N_C)
        for y in range(N_Y)
    ]
    return pl.pallas_call(
        gathered_proj_kernel,
        out_shape=jax.ShapeDtypeStruct((tokens, weight_v.shape[1]), jnp.bfloat16),
        grid=(N_Z // Z_PER_STEP,),
        scratch_shapes=[pltpu.VMEM((tokens, weight_v.shape[1]), jnp.float32)],
        in_specs=[pl.BlockSpec((step, tokens, width), lambda i: (i, 0, 0))] + w_specs,
        out_specs=pl.BlockSpec((tokens, weight_v.shape[1]), lambda i: (0, 0)),
    )(feats, *([weight_v] * step))


def on_device(inputs, queries, keys, w_value, w_out):
    activ = inputs[0]
    weight_v = w_value[0]
    weight_o = w_out[0]
    length = activ.shape[0]
    col_width = activ.shape[1]
    n_feat = weight_v.shape[0]

    core = lax.axis_index("tc").astype(jnp.int32).reshape(1)
    weight_from_sib = swap(pick_columns(1 - core, weight_o, col_width), "tc")
    y_first = lax.axis_index("ty") == 0
    other = swap(activ, "ty")
    gathered = jnp.stack([jnp.where(y_first, activ, other), jnp.where(y_first, other, activ)])
    gathered = lax.all_gather(gathered, ("tz", "tc"), axis=0)
    values = gathered_proj(gathered, weight_v)

    heads_here = weight_v.shape[1] // HEAD_SIZE
    query_rows = queries[0].reshape(length // LEN, LEN, heads_here, HEAD_SIZE)
    key_rows = keys[0].reshape(length // LEN, LEN, heads_here, HEAD_SIZE)
    value_rows = values.reshape(length // LEN, LEN, heads_here, HEAD_SIZE)
    scores = jnp.einsum(
        "bqhd,bkhd->bhqk", query_rows, key_rows, preferred_element_type=jnp.float32
    ) / jnp.sqrt(jnp.float32(HEAD_SIZE))
    rows = lax.broadcasted_iota(jnp.int32, (LEN, LEN), 0)
    cols = lax.broadcasted_iota(jnp.int32, (LEN, LEN), 1)
    scores = jnp.where((cols <= rows)[None, None], scores, jnp.float32(-1e30))
    top = jnp.max(scores, axis=-1, keepdims=True)
    expo = jnp.exp(scores - top)
    probs = (expo / jnp.sum(expo, axis=-1, keepdims=True)).astype(jnp.bfloat16)
    context = jnp.einsum(
        "bhqk,bkhd->bqhd", probs, value_rows, preferred_element_type=jnp.float32
    ).astype(jnp.bfloat16)
    context = context.reshape(length, heads_here * HEAD_SIZE)

    y_index = lax.axis_index("ty")
    own_group = (lax.axis_index("tz") * N_Y + y_index).astype(jnp.int32)
    sel = jnp.concatenate([core, own_group.reshape(1)])
    part = out_proj(sel, context, swap(context, "tc"), weight_from_sib, activ, weight_o, col_width)
    part = part.reshape(N_Z, N_Y, length, col_width)
    part = lax.psum_scatter(part, "tz", scatter_dimension=0, tiled=False)
    keep = lax.dynamic_index_in_dim(part, y_index, 0, keepdims=False)
    send = lax.dynamic_index_in_dim(part, 1 - y_index, 0, keepdims=False)
    across = lax.ppermute(send, ("section", "ty"), [(i, 3 - i) for i in range(4)])
    result = swap(keep, "section").astype(jnp.float32) + across.astype(jnp.float32)
    return result.astype(jnp.bfloat16)[None]


def solution(mesh):
    n_sec, n_dp, n_t = mesh.devices.shape
    sub = Mesh(
        mesh.devices.reshape(n_sec, n_dp, N_Z, N_Y, N_C),
        ("section", "dp", "tz", "ty", "tc"),
    )
    spec = P("section", "dp", ("tz", "ty", "tc"))
    return jax.shard_map(
        on_device,
        mesh=sub,
        in_specs=(
            spec,
            spec,
            spec,
            P("section", None, ("tz", "ty", "tc")),
            P("section", ("tz", "ty", "tc"), None),
        ),
        out_specs=spec,
        check_vma=False,
    )
```

```python
import jax
import jax.numpy as jnp
from jax import lax
from jax.experimental import pallas as pl
from jax.experimental.pallas import tpu as pltpu
from jax.sharding import Mesh
from jax.sharding import PartitionSpec as P

HEAD_SIZE = 128
LEN = 256
N_Z, N_Y, N_C = 8, 2, 2
GROUPS_PER_STEP = 8
Z_PER_STEP = 4


def swap(value, axis):
    return lax.ppermute(value, axis, [(0, 1), (1, 0)])


def column_spec(inner, width, step, k):
    return pl.BlockSpec((inner, width), lambda i, c: (0, N_C * (i * step + k) + c[0]))


def pick_kernel(sel_ref, *refs):
    w_refs, o_ref = refs[:-1], refs[-1]
    for k, w_ref in enumerate(w_refs):
        o_ref[k] = w_ref[...]


def pick_columns(sel, weight_o, width):
    inner = weight_o.shape[0]
    n_groups = weight_o.shape[1] // (N_C * width)
    step = GROUPS_PER_STEP
    return pl.pallas_call(
        pick_kernel,
        out_shape=jax.ShapeDtypeStruct((n_groups, inner, width), weight_o.dtype),
        grid_spec=pltpu.PrefetchScalarGridSpec(
            num_scalar_prefetch=1,
            grid=(n_groups // step,),
            in_specs=[column_spec(inner, width, step, k) for k in range(step)],
            out_specs=pl.BlockSpec((step, inner, width), lambda i, c: (i, 0, 0)),
        ),
    )(sel, *([weight_o] * step))


def out_proj_kernel(core_ref, ctx_ref, ctx_sib_ref, w_sib_ref, *refs):
    w_refs, o_ref = refs[:-1], refs[-1]
    ctx = ctx_ref[...]
    ctx_sib = ctx_sib_ref[...]
    for k, w_ref in enumerate(w_refs):
        d = jnp.dot(ctx, w_ref[...], preferred_element_type=jnp.float32)
        d = d + jnp.dot(ctx_sib, w_sib_ref[k], preferred_element_type=jnp.float32)
        o_ref[k] = d.astype(jnp.bfloat16)


def out_proj(core, context, context_sib, weight_sib, weight_o, width):
    tokens, inner = context.shape
    n_groups = weight_o.shape[1] // (N_C * width)
    step = GROUPS_PER_STEP
    return pl.pallas_call(
        out_proj_kernel,
        out_shape=jax.ShapeDtypeStruct((n_groups, tokens, width), jnp.bfloat16),
        grid_spec=pltpu.PrefetchScalarGridSpec(
            num_scalar_prefetch=1,
            grid=(n_groups // step,),
            in_specs=[
                pl.BlockSpec((tokens, inner), lambda i, c: (0, 0)),
                pl.BlockSpec((tokens, inner), lambda i, c: (0, 0)),
                pl.BlockSpec((step, inner, width), lambda i, c: (i, 0, 0)),
            ]
            + [column_spec(inner, width, step, k) for k in range(step)],
            out_specs=pl.BlockSpec((step, tokens, width), lambda i, c: (i, 0, 0)),
        ),
    )(core, context, context_sib, weight_sib, *([weight_o] * step))


def gathered_proj_kernel(f_ref, *refs):
    w_refs, o_ref = refs[:-1], refs[-1]

    @pl.when(pl.program_id(0) == 0)
    def _():
        o_ref[...] = jnp.zeros(o_ref.shape, o_ref.dtype)

    acc = o_ref[...]
    for k, w_ref in enumerate(w_refs):
        acc = acc + jnp.dot(f_ref[k], w_ref[...], preferred_element_type=jnp.float32)
    o_ref[...] = acc


def gathered_proj(feats, weight_v):
    tokens, width = feats.shape[-2:]
    feats = feats.reshape(-1, tokens, width)
    per_z = N_C * N_Y
    step = Z_PER_STEP * per_z
    w_specs = [
        pl.BlockSpec(
            (width, weight_v.shape[1]),
            lambda i, z=z, c=c, y=y: ((i * Z_PER_STEP + z) * per_z + y * N_C + c, 0),
        )
        for z in range(Z_PER_STEP)
        for c in range(N_C)
        for y in range(N_Y)
    ]
    return pl.pallas_call(
        gathered_proj_kernel,
        out_shape=jax.ShapeDtypeStruct((tokens, weight_v.shape[1]), jnp.float32),
        grid=(N_Z // Z_PER_STEP,),
        in_specs=[pl.BlockSpec((step, tokens, width), lambda i: (i, 0, 0))] + w_specs,
        out_specs=pl.BlockSpec((tokens, weight_v.shape[1]), lambda i: (0, 0)),
    )(feats, *([weight_v] * step))


def on_device(inputs, queries, keys, w_value, w_out):
    activ = inputs[0]
    weight_v = w_value[0]
    weight_o = w_out[0]
    length = activ.shape[0]
    col_width = activ.shape[1]
    n_feat = weight_v.shape[0]

    core = lax.axis_index("tc").astype(jnp.int32).reshape(1)
    weight_from_sib = swap(pick_columns(1 - core, weight_o, col_width), "tc")
    y_first = lax.axis_index("ty") == 0
    other = swap(activ, "ty")
    gathered = jnp.stack([jnp.where(y_first, activ, other), jnp.where(y_first, other, activ)])
    gathered = lax.all_gather(gathered, ("tz", "tc"), axis=0)
    values = gathered_proj(gathered, weight_v)
    values = values.astype(jnp.bfloat16)

    heads_here = weight_v.shape[1] // HEAD_SIZE
    query_rows = queries[0].reshape(length // LEN, LEN, heads_here, HEAD_SIZE)
    key_rows = keys[0].reshape(length // LEN, LEN, heads_here, HEAD_SIZE)
    value_rows = values.reshape(length // LEN, LEN, heads_here, HEAD_SIZE)
    scores = jnp.einsum(
        "bqhd,bkhd->bhqk", query_rows, key_rows, preferred_element_type=jnp.float32
    ) / jnp.sqrt(jnp.float32(HEAD_SIZE))
    rows = lax.broadcasted_iota(jnp.int32, (LEN, LEN), 0)
    cols = lax.broadcasted_iota(jnp.int32, (LEN, LEN), 1)
    scores = jnp.where((cols <= rows)[None, None], scores, jnp.float32(-1e30))
    top = jnp.max(scores, axis=-1, keepdims=True)
    expo = jnp.exp(scores - top)
    probs = (expo / jnp.sum(expo, axis=-1, keepdims=True)).astype(jnp.bfloat16)
    context = jnp.einsum(
        "bhqk,bkhd->bqhd", probs, value_rows, preferred_element_type=jnp.float32
    ).astype(jnp.bfloat16)
    context = context.reshape(length, heads_here * HEAD_SIZE)

    part = out_proj(core, context, swap(context, "tc"), weight_from_sib, weight_o, col_width)
    part = lax.psum_scatter(part, ("tz", "ty"), scatter_dimension=0, tiled=False)
    result = part.astype(jnp.float32) + activ.astype(jnp.float32)
    result = swap(result.astype(jnp.bfloat16), "section")
    return result.astype(jnp.bfloat16)[None]


def solution(mesh):
    n_sec, n_dp, n_t = mesh.devices.shape
    sub = Mesh(
        mesh.devices.reshape(n_sec, n_dp, N_Z, N_Y, N_C),
        ("section", "dp", "tz", "ty", "tc"),
    )
    spec = P("section", "dp", ("tz", "ty", "tc"))
    return jax.shard_map(
        on_device,
        mesh=sub,
        in_specs=(
            spec,
            spec,
            spec,
            P("section", None, ("tz", "ty", "tc")),
            P("section", ("tz", "ty", "tc"), None),
        ),
        out_specs=spec,
        check_vma=False,
    )
```

```python
import jax
import jax.numpy as jnp
from jax import lax
from jax.experimental import pallas as pl
from jax.experimental.pallas import tpu as pltpu
from jax.sharding import Mesh
from jax.sharding import PartitionSpec as P

HEAD_SIZE = 128
LEN = 256
N_Z, N_Y, N_C = 8, 2, 2
GROUPS_PER_STEP = 8
Z_PER_STEP = 4


def swap(value, axis):
    return lax.ppermute(value, axis, [(0, 1), (1, 0)])


def column_spec(inner, width, step, k):
    return pl.BlockSpec((inner, width), lambda i, c: (0, N_C * (i * step + k) + c[0]))


def pick_kernel(sel_ref, *refs):
    w_refs, o_ref = refs[:-1], refs[-1]
    for k, w_ref in enumerate(w_refs):
        o_ref[k] = w_ref[...]


def pick_columns(sel, weight_o, width):
    inner = weight_o.shape[0]
    n_groups = weight_o.shape[1] // (N_C * width)
    step = GROUPS_PER_STEP
    return pl.pallas_call(
        pick_kernel,
        out_shape=jax.ShapeDtypeStruct((n_groups, inner, width), weight_o.dtype),
        grid_spec=pltpu.PrefetchScalarGridSpec(
            num_scalar_prefetch=1,
            grid=(n_groups // step,),
            in_specs=[column_spec(inner, width, step, k) for k in range(step)],
            out_specs=pl.BlockSpec((step, inner, width), lambda i, c: (i, 0, 0)),
        ),
    )(sel, *([weight_o] * step))


def out_proj_kernel(core_ref, ctx_ref, ctx_sib_ref, w_sib_ref, *refs):
    w_refs, o_ref = refs[:-1], refs[-1]
    ctx = ctx_ref[...]
    ctx_sib = ctx_sib_ref[...]
    for k, w_ref in enumerate(w_refs):
        d = jnp.dot(ctx, w_ref[...], preferred_element_type=jnp.float32)
        d = d + jnp.dot(ctx_sib, w_sib_ref[k], preferred_element_type=jnp.float32)
        o_ref[k] = d.astype(jnp.bfloat16)


def out_proj(core, context, context_sib, weight_sib, weight_o, width):
    tokens, inner = context.shape
    n_groups = weight_o.shape[1] // (N_C * width)
    step = GROUPS_PER_STEP
    return pl.pallas_call(
        out_proj_kernel,
        out_shape=jax.ShapeDtypeStruct((n_groups, tokens, width), jnp.bfloat16),
        grid_spec=pltpu.PrefetchScalarGridSpec(
            num_scalar_prefetch=1,
            grid=(n_groups // step,),
            in_specs=[
                pl.BlockSpec((tokens, inner), lambda i, c: (0, 0)),
                pl.BlockSpec((tokens, inner), lambda i, c: (0, 0)),
                pl.BlockSpec((step, inner, width), lambda i, c: (i, 0, 0)),
            ]
            + [column_spec(inner, width, step, k) for k in range(step)],
            out_specs=pl.BlockSpec((step, tokens, width), lambda i, c: (i, 0, 0)),
        ),
    )(core, context, context_sib, weight_sib, *([weight_o] * step))


def gathered_proj_kernel(f_ref, w_ref, o_ref):
    width = f_ref.shape[-1]

    @pl.when(pl.program_id(0) == 0)
    def _():
        o_ref[...] = jnp.zeros(o_ref.shape, o_ref.dtype)

    acc = o_ref[...]
    for z in range(Z_PER_STEP):
        for c in range(N_C):
            for y in range(N_Y):
                slot = (z * N_C + c) * N_Y + y
                row = ((z * N_Y + y) * N_C + c) * width
                acc = acc + jnp.dot(
                    f_ref[slot], w_ref[row:row + width, :], preferred_element_type=jnp.float32
                )
    o_ref[...] = acc


def gathered_proj(feats, weight_v):
    tokens, width = feats.shape[-2:]
    feats = feats.reshape(-1, tokens, width)
    step = Z_PER_STEP * N_C * N_Y
    return pl.pallas_call(
        gathered_proj_kernel,
        out_shape=jax.ShapeDtypeStruct((tokens, weight_v.shape[1]), jnp.float32),
        grid=(N_Z // Z_PER_STEP,),
        in_specs=[
            pl.BlockSpec((step, tokens, width), lambda i: (i, 0, 0)),
            pl.BlockSpec((step * width, weight_v.shape[1]), lambda i: (i, 0)),
        ],
        out_specs=pl.BlockSpec((tokens, weight_v.shape[1]), lambda i: (0, 0)),
    )(feats, weight_v)


def on_device(inputs, queries, keys, w_value, w_out):
    activ = inputs[0]
    weight_v = w_value[0]
    weight_o = w_out[0]
    length = activ.shape[0]
    col_width = activ.shape[1]
    n_feat = weight_v.shape[0]

    core = lax.axis_index("tc").astype(jnp.int32).reshape(1)
    weight_from_sib = swap(pick_columns(1 - core, weight_o, col_width), "tc")
    y_first = lax.axis_index("ty") == 0
    other = swap(activ, "ty")
    gathered = jnp.stack([jnp.where(y_first, activ, other), jnp.where(y_first, other, activ)])
    gathered = lax.all_gather(gathered, ("tz", "tc"), axis=0)
    values = gathered_proj(gathered, weight_v)
    values = values.astype(jnp.bfloat16)

    heads_here = weight_v.shape[1] // HEAD_SIZE
    query_rows = queries[0].reshape(length // LEN, LEN, heads_here, HEAD_SIZE)
    key_rows = keys[0].reshape(length // LEN, LEN, heads_here, HEAD_SIZE)
    value_rows = values.reshape(length // LEN, LEN, heads_here, HEAD_SIZE)
    scores = jnp.einsum(
        "bqhd,bkhd->bhqk", query_rows, key_rows, preferred_element_type=jnp.float32
    ) / jnp.sqrt(jnp.float32(HEAD_SIZE))
    rows = lax.broadcasted_iota(jnp.int32, (LEN, LEN), 0)
    cols = lax.broadcasted_iota(jnp.int32, (LEN, LEN), 1)
    scores = jnp.where((cols <= rows)[None, None], scores, jnp.float32(-1e30))
    top = jnp.max(scores, axis=-1, keepdims=True)
    expo = jnp.exp(scores - top)
    probs = (expo / jnp.sum(expo, axis=-1, keepdims=True)).astype(jnp.bfloat16)
    context = jnp.einsum(
        "bhqk,bkhd->bqhd", probs, value_rows, preferred_element_type=jnp.float32
    ).astype(jnp.bfloat16)
    context = context.reshape(length, heads_here * HEAD_SIZE)

    part = out_proj(core, context, swap(context, "tc"), weight_from_sib, weight_o, col_width)
    part = part.reshape(N_Z, N_Y, length, col_width)
    part = lax.psum_scatter(part, "tz", scatter_dimension=0, tiled=False)
    y_index = lax.axis_index("ty")
    keep = lax.dynamic_index_in_dim(part, y_index, 0, keepdims=False)
    send = lax.dynamic_index_in_dim(part, 1 - y_index, 0, keepdims=False)
    keep = (keep.astype(jnp.float32) + activ.astype(jnp.float32)).astype(jnp.bfloat16)
    across = lax.ppermute(send, ("section", "ty"), [(i, 3 - i) for i in range(4)])
    result = swap(keep, "section").astype(jnp.float32) + across.astype(jnp.float32)
    return result.astype(jnp.bfloat16)[None]


def solution(mesh):
    n_sec, n_dp, n_t = mesh.devices.shape
    sub = Mesh(
        mesh.devices.reshape(n_sec, n_dp, N_Z, N_Y, N_C),
        ("section", "dp", "tz", "ty", "tc"),
    )
    spec = P("section", "dp", ("tz", "ty", "tc"))
    return jax.shard_map(
        on_device,
        mesh=sub,
        in_specs=(
            spec,
            spec,
            spec,
            P("section", None, ("tz", "ty", "tc")),
            P("section", ("tz", "ty", "tc"), None),
        ),
        out_specs=spec,
        check_vma=False,
    )
```

```python
import jax
import jax.numpy as jnp
from jax import lax
from jax.experimental import pallas as pl
from jax.experimental.pallas import tpu as pltpu
from jax.sharding import Mesh
from jax.sharding import PartitionSpec as P

HEAD_SIZE = 128
LEN = 256
N_Z, N_Y, N_C = 8, 2, 2
GROUPS_PER_STEP = 8
Z_PER_STEP = 4


def swap(value, axis):
    return lax.ppermute(value, axis, [(0, 1), (1, 0)])


def column_spec(inner, width, step, k):
    return pl.BlockSpec((inner, width), lambda i, c: (0, N_C * (i * step + k) + c[0]))


def pick_kernel(sel_ref, *refs):
    w_refs, o_ref = refs[:-1], refs[-1]
    for k, w_ref in enumerate(w_refs):
        o_ref[k] = w_ref[...]


def pick_columns(sel, weight_o, width):
    inner = weight_o.shape[0]
    n_groups = weight_o.shape[1] // (N_C * width)
    step = GROUPS_PER_STEP
    return pl.pallas_call(
        pick_kernel,
        out_shape=jax.ShapeDtypeStruct((n_groups, inner, width), weight_o.dtype),
        grid_spec=pltpu.PrefetchScalarGridSpec(
            num_scalar_prefetch=1,
            grid=(n_groups // step,),
            in_specs=[column_spec(inner, width, step, k) for k in range(step)],
            out_specs=pl.BlockSpec((step, inner, width), lambda i, c: (i, 0, 0)),
        ),
    )(sel, *([weight_o] * step))


def out_proj_kernel(core_ref, ctx_ref, ctx_sib_ref, w_sib_ref, *refs):
    w_refs, o_ref = refs[:-1], refs[-1]
    ctx = ctx_ref[...]
    ctx_sib = ctx_sib_ref[...]
    for k, w_ref in enumerate(w_refs):
        d = jnp.dot(ctx, w_ref[...], preferred_element_type=jnp.float32)
        d = d + jnp.dot(ctx_sib, w_sib_ref[k], preferred_element_type=jnp.float32)
        o_ref[k] = d.astype(jnp.bfloat16)


def out_proj(core, context, context_sib, weight_sib, weight_o, width):
    tokens, inner = context.shape
    n_groups = weight_o.shape[1] // (N_C * width)
    step = GROUPS_PER_STEP
    return pl.pallas_call(
        out_proj_kernel,
        out_shape=jax.ShapeDtypeStruct((n_groups, tokens, width), jnp.bfloat16),
        grid_spec=pltpu.PrefetchScalarGridSpec(
            num_scalar_prefetch=1,
            grid=(n_groups // step,),
            in_specs=[
                pl.BlockSpec((tokens, inner), lambda i, c: (0, 0)),
                pl.BlockSpec((tokens, inner), lambda i, c: (0, 0)),
                pl.BlockSpec((step, inner, width), lambda i, c: (i, 0, 0)),
            ]
            + [column_spec(inner, width, step, k) for k in range(step)],
            out_specs=pl.BlockSpec((step, tokens, width), lambda i, c: (i, 0, 0)),
        ),
    )(core, context, context_sib, weight_sib, *([weight_o] * step))


def gathered_proj_kernel(f_ref, w_ref, o_ref, acc_ref):
    width = f_ref.shape[-1]

    @pl.when(pl.program_id(0) == 0)
    def _():
        acc_ref[...] = jnp.zeros(acc_ref.shape, acc_ref.dtype)

    acc = acc_ref[...]
    for z in range(Z_PER_STEP):
        for c in range(N_C):
            for y in range(N_Y):
                slot = (z * N_C + c) * N_Y + y
                row = ((z * N_Y + y) * N_C + c) * width
                acc = acc + lax.dot_general(
                    w_ref[row:row + width, :],
                    f_ref[slot],
                    (((0,), (1,)), ((), ())),
                    preferred_element_type=jnp.float32,
                )
    acc_ref[...] = acc

    @pl.when(pl.program_id(0) == pl.num_programs(0) - 1)
    def _():
        o_ref[...] = acc.astype(o_ref.dtype)


def gathered_proj(feats, weight_v):
    tokens, width = feats.shape[-2:]
    feats = feats.reshape(-1, tokens, width)
    step = Z_PER_STEP * N_C * N_Y
    return pl.pallas_call(
        gathered_proj_kernel,
        out_shape=jax.ShapeDtypeStruct((weight_v.shape[1], tokens), jnp.bfloat16),
        grid=(N_Z // Z_PER_STEP,),
        in_specs=[
            pl.BlockSpec((step, tokens, width), lambda i: (i, 0, 0)),
            pl.BlockSpec((step * width, weight_v.shape[1]), lambda i: (i, 0)),
        ],
        out_specs=pl.BlockSpec((weight_v.shape[1], tokens), lambda i: (0, 0)),
        scratch_shapes=[pltpu.VMEM((weight_v.shape[1], tokens), jnp.float32)],
    )(feats, weight_v)


def on_device(inputs, queries, keys, w_value, w_out):
    activ = inputs[0]
    weight_v = w_value[0]
    weight_o = w_out[0]
    length = activ.shape[0]
    col_width = activ.shape[1]
    n_feat = weight_v.shape[0]

    core = lax.axis_index("tc").astype(jnp.int32).reshape(1)
    weight_from_sib = swap(pick_columns(1 - core, weight_o, col_width), "tc")
    y_first = lax.axis_index("ty") == 0
    other = swap(activ, "ty")
    gathered = jnp.stack([jnp.where(y_first, activ, other), jnp.where(y_first, other, activ)])
    gathered = lax.all_gather(gathered, ("tz", "tc"), axis=0)
    values = gathered_proj(gathered, weight_v).T

    heads_here = weight_v.shape[1] // HEAD_SIZE
    query_rows = queries[0].reshape(length // LEN, LEN, heads_here, HEAD_SIZE)
    key_rows = keys[0].reshape(length // LEN, LEN, heads_here, HEAD_SIZE)
    value_rows = values.reshape(length // LEN, LEN, heads_here, HEAD_SIZE)
    scores = jnp.einsum(
        "bqhd,bkhd->bhqk", query_rows, key_rows, preferred_element_type=jnp.float32
    ) / jnp.sqrt(jnp.float32(HEAD_SIZE))
    rows = lax.broadcasted_iota(jnp.int32, (LEN, LEN), 0)
    cols = lax.broadcasted_iota(jnp.int32, (LEN, LEN), 1)
    scores = jnp.where((cols <= rows)[None, None], scores, jnp.float32(-1e30))
    top = jnp.max(scores, axis=-1, keepdims=True)
    expo = jnp.exp(scores - top)
    probs = (expo / jnp.sum(expo, axis=-1, keepdims=True)).astype(jnp.bfloat16)
    context = jnp.einsum(
        "bhqk,bkhd->bqhd", probs, value_rows, preferred_element_type=jnp.float32
    ).astype(jnp.bfloat16)
    context = context.reshape(length, heads_here * HEAD_SIZE)

    part = out_proj(core, context, swap(context, "tc"), weight_from_sib, weight_o, col_width)
    part = part.reshape(N_Z, N_Y, length, col_width)
    part = lax.psum_scatter(part, "tz", scatter_dimension=0, tiled=False)
    y_index = lax.axis_index("ty")
    keep = lax.dynamic_index_in_dim(part, y_index, 0, keepdims=False)
    send = lax.dynamic_index_in_dim(part, 1 - y_index, 0, keepdims=False)
    keep = (keep.astype(jnp.float32) + activ.astype(jnp.float32)).astype(jnp.bfloat16)
    across = lax.ppermute(send, ("section", "ty"), [(i, 3 - i) for i in range(4)])
    result = swap(keep, "section").astype(jnp.float32) + across.astype(jnp.float32)
    return result.astype(jnp.bfloat16)[None]


def solution(mesh):
    n_sec, n_dp, n_t = mesh.devices.shape
    sub = Mesh(
        mesh.devices.reshape(n_sec, n_dp, N_Z, N_Y, N_C),
        ("section", "dp", "tz", "ty", "tc"),
    )
    spec = P("section", "dp", ("tz", "ty", "tc"))
    return jax.shard_map(
        on_device,
        mesh=sub,
        in_specs=(
            spec,
            spec,
            spec,
            P("section", None, ("tz", "ty", "tc")),
            P("section", ("tz", "ty", "tc"), None),
        ),
        out_specs=spec,
        check_vma=False,
    )
```

```python
import jax
import jax.numpy as jnp
from jax import lax
from jax.experimental import pallas as pl
from jax.experimental.pallas import tpu as pltpu
from jax.sharding import Mesh
from jax.sharding import PartitionSpec as P

HEAD_SIZE = 128
LEN = 256
N_Z, N_Y, N_C = 8, 2, 2
GROUPS_PER_STEP = 8
Z_PER_STEP = 4


def swap(value, axis):
    return lax.ppermute(value, axis, [(0, 1), (1, 0)])


def column_spec(inner, width, step, k):
    return pl.BlockSpec((inner, width), lambda i, c: (0, N_C * (i * step + k) + c[0]))


def pick_kernel(sel_ref, *refs):
    w_refs, o_ref = refs[:-1], refs[-1]
    for k, w_ref in enumerate(w_refs):
        o_ref[k] = w_ref[...]


def pick_columns(sel, weight_o, width):
    inner = weight_o.shape[0]
    n_groups = weight_o.shape[1] // (N_C * width)
    step = GROUPS_PER_STEP
    return pl.pallas_call(
        pick_kernel,
        out_shape=jax.ShapeDtypeStruct((n_groups, inner, width), weight_o.dtype),
        grid_spec=pltpu.PrefetchScalarGridSpec(
            num_scalar_prefetch=1,
            grid=(n_groups // step,),
            in_specs=[column_spec(inner, width, step, k) for k in range(step)],
            out_specs=pl.BlockSpec((step, inner, width), lambda i, c: (i, 0, 0)),
        ),
    )(sel, *([weight_o] * step))


def out_proj_kernel(core_ref, ctx_ref, ctx_sib_ref, w_sib_ref, *refs):
    w_refs, o_ref = refs[:-1], refs[-1]
    ctx = ctx_ref[...]
    ctx_sib = ctx_sib_ref[...]
    dims = (((0,), (0,)), ((), ()))
    for k, w_ref in enumerate(w_refs):
        d = lax.dot_general(ctx, w_ref[...], dims, preferred_element_type=jnp.float32)
        d = d + lax.dot_general(ctx_sib, w_sib_ref[k], dims, preferred_element_type=jnp.float32)
        o_ref[k] = d.astype(jnp.bfloat16)


def out_proj(core, context, context_sib, weight_sib, weight_o, width):
    inner, tokens = context.shape
    n_groups = weight_o.shape[1] // (N_C * width)
    step = GROUPS_PER_STEP
    return pl.pallas_call(
        out_proj_kernel,
        out_shape=jax.ShapeDtypeStruct((n_groups, tokens, width), jnp.bfloat16),
        grid_spec=pltpu.PrefetchScalarGridSpec(
            num_scalar_prefetch=1,
            grid=(n_groups // step,),
            in_specs=[
                pl.BlockSpec((inner, tokens), lambda i, c: (0, 0)),
                pl.BlockSpec((inner, tokens), lambda i, c: (0, 0)),
                pl.BlockSpec((step, inner, width), lambda i, c: (i, 0, 0)),
            ]
            + [column_spec(inner, width, step, k) for k in range(step)],
            out_specs=pl.BlockSpec((step, tokens, width), lambda i, c: (i, 0, 0)),
        ),
    )(core, context, context_sib, weight_sib, *([weight_o] * step))


def gathered_proj_kernel(f_ref, w_ref, o_ref, acc_ref):
    width = f_ref.shape[-1]

    @pl.when(pl.program_id(0) == 0)
    def _():
        acc_ref[...] = jnp.zeros(acc_ref.shape, acc_ref.dtype)

    acc = acc_ref[...]
    for z in range(Z_PER_STEP):
        for c in range(N_C):
            for y in range(N_Y):
                slot = (z * N_C + c) * N_Y + y
                row = ((z * N_Y + y) * N_C + c) * width
                acc = acc + lax.dot_general(
                    w_ref[row:row + width, :],
                    f_ref[slot],
                    (((0,), (1,)), ((), ())),
                    preferred_element_type=jnp.float32,
                )
    acc_ref[...] = acc

    @pl.when(pl.program_id(0) == pl.num_programs(0) - 1)
    def _():
        o_ref[...] = acc.astype(o_ref.dtype)


def gathered_proj(feats, weight_v):
    tokens, width = feats.shape[-2:]
    feats = feats.reshape(-1, tokens, width)
    step = Z_PER_STEP * N_C * N_Y
    return pl.pallas_call(
        gathered_proj_kernel,
        out_shape=jax.ShapeDtypeStruct((weight_v.shape[1], tokens), jnp.bfloat16),
        grid=(N_Z // Z_PER_STEP,),
        in_specs=[
            pl.BlockSpec((step, tokens, width), lambda i: (i, 0, 0)),
            pl.BlockSpec((step * width, weight_v.shape[1]), lambda i: (i, 0)),
        ],
        out_specs=pl.BlockSpec((weight_v.shape[1], tokens), lambda i: (0, 0)),
        scratch_shapes=[pltpu.VMEM((weight_v.shape[1], tokens), jnp.float32)],
    )(feats, weight_v)


def on_device(inputs, queries, keys, w_value, w_out):
    activ = inputs[0]
    weight_v = w_value[0]
    weight_o = w_out[0]
    length = activ.shape[0]
    col_width = activ.shape[1]
    n_feat = weight_v.shape[0]

    core = lax.axis_index("tc").astype(jnp.int32).reshape(1)
    weight_from_sib = swap(pick_columns(1 - core, weight_o, col_width), "tc")
    y_first = lax.axis_index("ty") == 0
    other = swap(activ, "ty")
    gathered = jnp.stack([jnp.where(y_first, activ, other), jnp.where(y_first, other, activ)])
    gathered = lax.all_gather(gathered, ("tz", "tc"), axis=0)
    values = gathered_proj(gathered, weight_v).T

    heads_here = weight_v.shape[1] // HEAD_SIZE
    query_rows = queries[0].reshape(length // LEN, LEN, heads_here, HEAD_SIZE)
    key_rows = keys[0].reshape(length // LEN, LEN, heads_here, HEAD_SIZE)
    value_rows = values.reshape(length // LEN, LEN, heads_here, HEAD_SIZE)
    scores = jnp.einsum(
        "bqhd,bkhd->bhqk", query_rows, key_rows, preferred_element_type=jnp.float32
    ) / jnp.sqrt(jnp.float32(HEAD_SIZE))
    rows = lax.broadcasted_iota(jnp.int32, (LEN, LEN), 0)
    cols = lax.broadcasted_iota(jnp.int32, (LEN, LEN), 1)
    scores = jnp.where((cols <= rows)[None, None], scores, jnp.float32(-1e30))
    top = jnp.max(scores, axis=-1, keepdims=True)
    expo = jnp.exp(scores - top)
    probs = (expo / jnp.sum(expo, axis=-1, keepdims=True)).astype(jnp.bfloat16)
    context = jnp.einsum(
        "bhqk,bkhd->bhdq", probs, value_rows, preferred_element_type=jnp.float32
    ).astype(jnp.bfloat16)
    context = context.reshape(heads_here * HEAD_SIZE, length)

    part = out_proj(core, context, swap(context, "tc"), weight_from_sib, weight_o, col_width)
    part = part.reshape(N_Z, N_Y, length, col_width)
    part = lax.psum_scatter(part, "tz", scatter_dimension=0, tiled=False)
    y_index = lax.axis_index("ty")
    keep = lax.dynamic_index_in_dim(part, y_index, 0, keepdims=False)
    send = lax.dynamic_index_in_dim(part, 1 - y_index, 0, keepdims=False)
    keep = (keep.astype(jnp.float32) + activ.astype(jnp.float32)).astype(jnp.bfloat16)
    across = lax.ppermute(send, ("section", "ty"), [(i, 3 - i) for i in range(4)])
    result = swap(keep, "section").astype(jnp.float32) + across.astype(jnp.float32)
    return result.astype(jnp.bfloat16)[None]


def solution(mesh):
    n_sec, n_dp, n_t = mesh.devices.shape
    sub = Mesh(
        mesh.devices.reshape(n_sec, n_dp, N_Z, N_Y, N_C),
        ("section", "dp", "tz", "ty", "tc"),
    )
    spec = P("section", "dp", ("tz", "ty", "tc"))
    return jax.shard_map(
        on_device,
        mesh=sub,
        in_specs=(
            spec,
            spec,
            spec,
            P("section", None, ("tz", "ty", "tc")),
            P("section", ("tz", "ty", "tc"), None),
        ),
        out_specs=spec,
        check_vma=False,
    )
```

```python
import jax
import jax.numpy as jnp
from jax import lax
from jax.experimental import pallas as pl
from jax.experimental.pallas import tpu as pltpu
from jax.sharding import Mesh
from jax.sharding import PartitionSpec as P

HEAD_SIZE = 128
LEN = 256
N_Z, N_Y, N_C = 8, 2, 2
GROUPS_PER_STEP = 8
Z_PER_STEP = 4


def swap(value, axis):
    return lax.ppermute(value, axis, [(0, 1), (1, 0)])


def column_spec(inner, width, step, k):
    return pl.BlockSpec((inner, width), lambda i, c: (0, N_C * (i * step + k) + c[0]))


def pick_kernel(sel_ref, *refs):
    w_refs, o_ref = refs[:-1], refs[-1]
    for k, w_ref in enumerate(w_refs):
        o_ref[k] = w_ref[...]


def pick_columns(sel, weight_o, width):
    inner = weight_o.shape[0]
    n_groups = weight_o.shape[1] // (N_C * width)
    step = GROUPS_PER_STEP
    return pl.pallas_call(
        pick_kernel,
        out_shape=jax.ShapeDtypeStruct((n_groups, inner, width), weight_o.dtype),
        grid_spec=pltpu.PrefetchScalarGridSpec(
            num_scalar_prefetch=1,
            grid=(n_groups // step,),
            in_specs=[column_spec(inner, width, step, k) for k in range(step)],
            out_specs=pl.BlockSpec((step, inner, width), lambda i, c: (i, 0, 0)),
        ),
    )(sel, *([weight_o] * step))


def out_proj_kernel(core_ref, ctx_ref, ctx_sib_ref, w_sib_ref, *refs):
    w_refs, o_ref = refs[:-1], refs[-1]
    ctx = ctx_ref[...]
    ctx_sib = ctx_sib_ref[...]
    for k, w_ref in enumerate(w_refs):
        d = jnp.dot(ctx, w_ref[...], preferred_element_type=jnp.float32)
        d = d + jnp.dot(ctx_sib, w_sib_ref[k], preferred_element_type=jnp.float32)
        o_ref[k] = d.astype(jnp.bfloat16)


def out_proj(core, context, context_sib, weight_sib, weight_o, width):
    tokens, inner = context.shape
    n_groups = weight_o.shape[1] // (N_C * width)
    step = GROUPS_PER_STEP
    return pl.pallas_call(
        out_proj_kernel,
        out_shape=jax.ShapeDtypeStruct((n_groups, tokens, width), jnp.bfloat16),
        grid_spec=pltpu.PrefetchScalarGridSpec(
            num_scalar_prefetch=1,
            grid=(n_groups // step,),
            in_specs=[
                pl.BlockSpec((tokens, inner), lambda i, c: (0, 0)),
                pl.BlockSpec((tokens, inner), lambda i, c: (0, 0)),
                pl.BlockSpec((step, inner, width), lambda i, c: (i, 0, 0)),
            ]
            + [column_spec(inner, width, step, k) for k in range(step)],
            out_specs=pl.BlockSpec((step, tokens, width), lambda i, c: (i, 0, 0)),
        ),
    )(core, context, context_sib, weight_sib, *([weight_o] * step))


def gathered_proj_kernel(f_ref, w_ref, o_ref, acc_ref):
    width = f_ref.shape[-1]

    @pl.when(pl.program_id(0) == 0)
    def _():
        acc_ref[...] = jnp.zeros(acc_ref.shape, acc_ref.dtype)

    acc = acc_ref[...]
    for z in range(Z_PER_STEP):
        for c in range(N_C):
            for y in range(N_Y):
                slot = (z * N_C + c) * N_Y + y
                row = ((z * N_Y + y) * N_C + c) * width
                acc = acc + lax.dot_general(
                    w_ref[row:row + width, :],
                    f_ref[slot],
                    (((0,), (1,)), ((), ())),
                    preferred_element_type=jnp.float32,
                )
    acc_ref[...] = acc

    @pl.when(pl.program_id(0) == pl.num_programs(0) - 1)
    def _():
        o_ref[...] = acc.astype(o_ref.dtype)


def gathered_proj(feats, weight_v):
    tokens, width = feats.shape[-2:]
    feats = feats.reshape(-1, tokens, width)
    step = Z_PER_STEP * N_C * N_Y
    return pl.pallas_call(
        gathered_proj_kernel,
        out_shape=jax.ShapeDtypeStruct((weight_v.shape[1], tokens), jnp.bfloat16),
        grid=(N_Z // Z_PER_STEP,),
        in_specs=[
            pl.BlockSpec((step, tokens, width), lambda i: (i, 0, 0)),
            pl.BlockSpec((step * width, weight_v.shape[1]), lambda i: (i, 0)),
        ],
        out_specs=pl.BlockSpec((weight_v.shape[1], tokens), lambda i: (0, 0)),
        scratch_shapes=[pltpu.VMEM((weight_v.shape[1], tokens), jnp.float32)],
    )(feats, weight_v)


def on_device(inputs, queries, keys, w_value, w_out):
    activ = inputs[0]
    weight_v = w_value[0]
    weight_o = w_out[0]
    length = activ.shape[0]
    col_width = activ.shape[1]
    n_feat = weight_v.shape[0]

    core = lax.axis_index("tc").astype(jnp.int32).reshape(1)
    weight_from_sib = swap(pick_columns(1 - core, weight_o, col_width), "tc")
    y_first = lax.axis_index("ty") == 0
    other = swap(activ, "ty")
    gathered = jnp.stack([jnp.where(y_first, activ, other), jnp.where(y_first, other, activ)])
    gathered = lax.all_gather(gathered, ("tz", "tc"), axis=0)
    values = gathered_proj(gathered, weight_v).T

    heads_here = weight_v.shape[1] // HEAD_SIZE
    query_rows = queries[0].reshape(length // LEN, LEN, heads_here, HEAD_SIZE)
    key_rows = keys[0].reshape(length // LEN, LEN, heads_here, HEAD_SIZE)
    value_rows = values.reshape(length // LEN, LEN, heads_here, HEAD_SIZE)
    scores = jnp.einsum(
        "bqhd,bkhd->bhqk", query_rows, key_rows, preferred_element_type=jnp.float32
    ) / jnp.sqrt(jnp.float32(HEAD_SIZE))
    rows = lax.broadcasted_iota(jnp.int32, (LEN, LEN), 0)
    cols = lax.broadcasted_iota(jnp.int32, (LEN, LEN), 1)
    scores = jnp.where((cols <= rows)[None, None], scores, jnp.float32(-1e30))
    top = jnp.max(scores, axis=-1, keepdims=True)
    expo = jnp.exp(scores - top)
    probs = (expo / jnp.sum(expo, axis=-1, keepdims=True)).astype(jnp.bfloat16)
    context = jnp.einsum(
        "bhqk,bkhd->bqhd", probs, value_rows, preferred_element_type=jnp.float32
    ).astype(jnp.bfloat16)
    context = context.reshape(length, heads_here * HEAD_SIZE)

    part = out_proj(core, context, swap(context, "tc"), weight_from_sib, weight_o, col_width)
    y_index = lax.axis_index("ty")
    own = lax.axis_index("tz") * N_Y + y_index
    own_sum = lax.dynamic_index_in_dim(part, own, 0, keepdims=False).astype(jnp.float32)
    own_sum = (own_sum + activ.astype(jnp.float32)).astype(jnp.bfloat16)
    part = lax.dynamic_update_index_in_dim(part, own_sum, own, 0)
    part = part.reshape(N_Z, N_Y, length, col_width)
    part = lax.psum_scatter(part, "tz", scatter_dimension=0, tiled=False)
    keep = lax.dynamic_index_in_dim(part, y_index, 0, keepdims=False)
    send = lax.dynamic_index_in_dim(part, 1 - y_index, 0, keepdims=False)
    across = lax.ppermute(send, ("section", "ty"), [(i, 3 - i) for i in range(4)])
    result = swap(keep, "section").astype(jnp.float32) + across.astype(jnp.float32)
    return result.astype(jnp.bfloat16)[None]


def solution(mesh):
    n_sec, n_dp, n_t = mesh.devices.shape
    sub = Mesh(
        mesh.devices.reshape(n_sec, n_dp, N_Z, N_Y, N_C),
        ("section", "dp", "tz", "ty", "tc"),
    )
    spec = P("section", "dp", ("tz", "ty", "tc"))
    return jax.shard_map(
        on_device,
        mesh=sub,
        in_specs=(
            spec,
            spec,
            spec,
            P("section", None, ("tz", "ty", "tc")),
            P("section", ("tz", "ty", "tc"), None),
        ),
        out_specs=spec,
        check_vma=False,
    )
```

```python
import jax
import jax.numpy as jnp
from jax import lax
from jax.experimental import pallas as pl
from jax.experimental.pallas import tpu as pltpu
from jax.sharding import Mesh
from jax.sharding import PartitionSpec as P

HEAD_SIZE = 128
LEN = 256
N_Z, N_Y, N_C = 8, 2, 2
GROUPS_PER_STEP = 16
Z_PER_STEP = 8


def swap(value, axis):
    return lax.ppermute(value, axis, [(0, 1), (1, 0)])


def column_spec(inner, width, step, k):
    return pl.BlockSpec((inner, width), lambda i, c: (0, N_C * (i * step + k) + c[0]))


def pick_kernel(sel_ref, *refs):
    w_refs, o_ref = refs[:-1], refs[-1]
    for k, w_ref in enumerate(w_refs):
        o_ref[k] = w_ref[...]


def pick_columns(sel, weight_o, width):
    inner = weight_o.shape[0]
    n_groups = weight_o.shape[1] // (N_C * width)
    step = GROUPS_PER_STEP
    return pl.pallas_call(
        pick_kernel,
        out_shape=jax.ShapeDtypeStruct((n_groups, inner, width), weight_o.dtype),
        grid_spec=pltpu.PrefetchScalarGridSpec(
            num_scalar_prefetch=1,
            grid=(n_groups // step,),
            in_specs=[column_spec(inner, width, step, k) for k in range(step)],
            out_specs=pl.BlockSpec((step, inner, width), lambda i, c: (i, 0, 0)),
        ),
    )(sel, *([weight_o] * step))


def out_proj_kernel(core_ref, ctx_ref, ctx_sib_ref, w_sib_ref, *refs):
    w_refs, o_ref = refs[:-1], refs[-1]
    ctx = ctx_ref[...]
    ctx_sib = ctx_sib_ref[...]
    for k, w_ref in enumerate(w_refs):
        d = jnp.dot(ctx, w_ref[...], preferred_element_type=jnp.float32)
        d = d + jnp.dot(ctx_sib, w_sib_ref[k], preferred_element_type=jnp.float32)
        o_ref[k] = d.astype(jnp.bfloat16)


def out_proj(core, context, context_sib, weight_sib, weight_o, width):
    tokens, inner = context.shape
    n_groups = weight_o.shape[1] // (N_C * width)
    step = GROUPS_PER_STEP
    return pl.pallas_call(
        out_proj_kernel,
        out_shape=jax.ShapeDtypeStruct((n_groups, tokens, width), jnp.bfloat16),
        grid_spec=pltpu.PrefetchScalarGridSpec(
            num_scalar_prefetch=1,
            grid=(n_groups // step,),
            in_specs=[
                pl.BlockSpec((tokens, inner), lambda i, c: (0, 0)),
                pl.BlockSpec((tokens, inner), lambda i, c: (0, 0)),
                pl.BlockSpec((step, inner, width), lambda i, c: (i, 0, 0)),
            ]
            + [column_spec(inner, width, step, k) for k in range(step)],
            out_specs=pl.BlockSpec((step, tokens, width), lambda i, c: (i, 0, 0)),
        ),
    )(core, context, context_sib, weight_sib, *([weight_o] * step))


def gathered_proj_kernel(f_ref, w_ref, o_ref, acc_ref):
    width = f_ref.shape[-1]

    @pl.when(pl.program_id(0) == 0)
    def _():
        acc_ref[...] = jnp.zeros(acc_ref.shape, acc_ref.dtype)

    acc = acc_ref[...]
    for z in range(Z_PER_STEP):
        for c in range(N_C):
            for y in range(N_Y):
                slot = (z * N_C + c) * N_Y + y
                row = ((z * N_Y + y) * N_C + c) * width
                acc = acc + lax.dot_general(
                    w_ref[row:row + width, :],
                    f_ref[slot],
                    (((0,), (1,)), ((), ())),
                    preferred_element_type=jnp.float32,
                )
    acc_ref[...] = acc

    @pl.when(pl.program_id(0) == pl.num_programs(0) - 1)
    def _():
        o_ref[...] = acc.astype(o_ref.dtype)


def gathered_proj(feats, weight_v):
    tokens, width = feats.shape[-2:]
    feats = feats.reshape(-1, tokens, width)
    step = Z_PER_STEP * N_C * N_Y
    return pl.pallas_call(
        gathered_proj_kernel,
        out_shape=jax.ShapeDtypeStruct((weight_v.shape[1], tokens), jnp.bfloat16),
        grid=(N_Z // Z_PER_STEP,),
        in_specs=[
            pl.BlockSpec((step, tokens, width), lambda i: (i, 0, 0)),
            pl.BlockSpec((step * width, weight_v.shape[1]), lambda i: (i, 0)),
        ],
        out_specs=pl.BlockSpec((weight_v.shape[1], tokens), lambda i: (0, 0)),
        scratch_shapes=[pltpu.VMEM((weight_v.shape[1], tokens), jnp.float32)],
    )(feats, weight_v)


def on_device(inputs, queries, keys, w_value, w_out):
    activ = inputs[0]
    weight_v = w_value[0]
    weight_o = w_out[0]
    length = activ.shape[0]
    col_width = activ.shape[1]
    n_feat = weight_v.shape[0]

    core = lax.axis_index("tc").astype(jnp.int32).reshape(1)
    weight_from_sib = swap(pick_columns(1 - core, weight_o, col_width), "tc")
    y_first = lax.axis_index("ty") == 0
    other = swap(activ, "ty")
    gathered = jnp.stack([jnp.where(y_first, activ, other), jnp.where(y_first, other, activ)])
    gathered = lax.all_gather(gathered, ("tz", "tc"), axis=0)
    values = gathered_proj(gathered, weight_v).T

    heads_here = weight_v.shape[1] // HEAD_SIZE
    query_rows = queries[0].reshape(length // LEN, LEN, heads_here, HEAD_SIZE)
    key_rows = keys[0].reshape(length // LEN, LEN, heads_here, HEAD_SIZE)
    value_rows = values.reshape(length // LEN, LEN, heads_here, HEAD_SIZE)
    scores = jnp.einsum(
        "bqhd,bkhd->bhqk", query_rows, key_rows, preferred_element_type=jnp.float32
    ) / jnp.sqrt(jnp.float32(HEAD_SIZE))
    rows = lax.broadcasted_iota(jnp.int32, (LEN, LEN), 0)
    cols = lax.broadcasted_iota(jnp.int32, (LEN, LEN), 1)
    scores = jnp.where((cols <= rows)[None, None], scores, jnp.float32(-1e30))
    top = jnp.max(scores, axis=-1, keepdims=True)
    expo = jnp.exp(scores - top)
    probs = (expo / jnp.sum(expo, axis=-1, keepdims=True)).astype(jnp.bfloat16)
    context = jnp.einsum(
        "bhqk,bkhd->bqhd", probs, value_rows, preferred_element_type=jnp.float32
    ).astype(jnp.bfloat16)
    context = context.reshape(length, heads_here * HEAD_SIZE)

    part = out_proj(core, context, swap(context, "tc"), weight_from_sib, weight_o, col_width)
    part = part.reshape(N_Z, N_Y, length, col_width)
    part = lax.psum_scatter(part, "tz", scatter_dimension=0, tiled=False)
    y_index = lax.axis_index("ty")
    keep = lax.dynamic_index_in_dim(part, y_index, 0, keepdims=False)
    send = lax.dynamic_index_in_dim(part, 1 - y_index, 0, keepdims=False)
    keep = (keep.astype(jnp.float32) + activ.astype(jnp.float32)).astype(jnp.bfloat16)
    across = lax.ppermute(send, ("section", "ty"), [(i, 3 - i) for i in range(4)])
    result = swap(keep, "section").astype(jnp.float32) + across.astype(jnp.float32)
    return result.astype(jnp.bfloat16)[None]


def solution(mesh):
    n_sec, n_dp, n_t = mesh.devices.shape
    sub = Mesh(
        mesh.devices.reshape(n_sec, n_dp, N_Z, N_Y, N_C),
        ("section", "dp", "tz", "ty", "tc"),
    )
    spec = P("section", "dp", ("tz", "ty", "tc"))
    return jax.shard_map(
        on_device,
        mesh=sub,
        in_specs=(
            spec,
            spec,
            spec,
            P("section", None, ("tz", "ty", "tc")),
            P("section", ("tz", "ty", "tc"), None),
        ),
        out_specs=spec,
        check_vma=False,
    )
```

```python
import jax
import jax.numpy as jnp
from jax import lax
from jax.experimental import pallas as pl
from jax.experimental.pallas import tpu as pltpu
from jax.sharding import Mesh
from jax.sharding import PartitionSpec as P

HEAD_SIZE = 128
LEN = 256
N_Z, N_Y, N_C = 8, 2, 2
GROUPS_PER_STEP = 8
Z_PER_STEP = 4


def swap(value, axis):
    return lax.ppermute(value, axis, [(0, 1), (1, 0)])


def column_spec(inner, width, step, k):
    return pl.BlockSpec((inner, width), lambda i, c: (0, N_C * (i * step + k) + c[0]))


def pick_kernel(sel_ref, *refs):
    w_refs, o_ref = refs[:-1], refs[-1]
    for k, w_ref in enumerate(w_refs):
        o_ref[k] = w_ref[...]


def pick_columns(sel, weight_o, width):
    inner = weight_o.shape[0]
    n_groups = weight_o.shape[1] // (N_C * width)
    step = GROUPS_PER_STEP
    return pl.pallas_call(
        pick_kernel,
        out_shape=jax.ShapeDtypeStruct((n_groups, inner, width), weight_o.dtype),
        grid_spec=pltpu.PrefetchScalarGridSpec(
            num_scalar_prefetch=1,
            grid=(n_groups // step,),
            in_specs=[column_spec(inner, width, step, k) for k in range(step)],
            out_specs=pl.BlockSpec((step, inner, width), lambda i, c: (i, 0, 0)),
        ),
    )(sel, *([weight_o] * step))


def out_proj_kernel(core_ref, ctx_ref, ctx_sib_ref, w_sib_ref, *refs):
    w_refs, o_ref = refs[:-1], refs[-1]
    ctx = ctx_ref[...]
    ctx_sib = ctx_sib_ref[...]
    for k, w_ref in enumerate(w_refs):
        d = jnp.dot(ctx, w_ref[...], preferred_element_type=jnp.float32)
        d = d + jnp.dot(ctx_sib, w_sib_ref[k], preferred_element_type=jnp.float32)
        o_ref[k] = d.astype(jnp.bfloat16)


def out_proj(core, context, context_sib, weight_sib, weight_o, width):
    tokens, inner = context.shape
    n_groups = weight_o.shape[1] // (N_C * width)
    step = GROUPS_PER_STEP
    return pl.pallas_call(
        out_proj_kernel,
        out_shape=jax.ShapeDtypeStruct((n_groups, tokens, width), jnp.bfloat16),
        grid_spec=pltpu.PrefetchScalarGridSpec(
            num_scalar_prefetch=1,
            grid=(n_groups // step,),
            in_specs=[
                pl.BlockSpec((tokens, inner), lambda i, c: (0, 0)),
                pl.BlockSpec((tokens, inner), lambda i, c: (0, 0)),
                pl.BlockSpec((step, inner, width), lambda i, c: (i, 0, 0)),
            ]
            + [column_spec(inner, width, step, k) for k in range(step)],
            out_specs=pl.BlockSpec((step, tokens, width), lambda i, c: (i, 0, 0)),
        ),
    )(core, context, context_sib, weight_sib, *([weight_o] * step))


def gathered_proj_kernel(f_ref, w_ref, o_ref, acc_ref):
    width = f_ref.shape[-1]

    @pl.when(pl.program_id(0) == 0)
    def _():
        acc_ref[...] = jnp.zeros(acc_ref.shape, acc_ref.dtype)

    acc = acc_ref[...]
    for z in range(Z_PER_STEP):
        for c in range(N_C):
            for y in range(N_Y):
                slot = (z * N_C + c) * N_Y + y
                row = ((z * N_Y + y) * N_C + c) * width
                acc = acc + lax.dot_general(
                    w_ref[row:row + width, :],
                    f_ref[slot],
                    (((0,), (1,)), ((), ())),
                    preferred_element_type=jnp.float32,
                )
    acc_ref[...] = acc

    @pl.when(pl.program_id(0) == pl.num_programs(0) - 1)
    def _():
        o_ref[...] = acc.astype(o_ref.dtype)


def gathered_proj(feats, weight_v):
    tokens, width = feats.shape[-2:]
    feats = feats.reshape(-1, tokens, width)
    step = Z_PER_STEP * N_C * N_Y
    return pl.pallas_call(
        gathered_proj_kernel,
        out_shape=jax.ShapeDtypeStruct((weight_v.shape[1], tokens), jnp.bfloat16),
        grid=(N_Z // Z_PER_STEP,),
        in_specs=[
            pl.BlockSpec((step, tokens, width), lambda i: (i, 0, 0)),
            pl.BlockSpec((step * width, weight_v.shape[1]), lambda i: (i, 0)),
        ],
        out_specs=pl.BlockSpec((weight_v.shape[1], tokens), lambda i: (0, 0)),
        scratch_shapes=[pltpu.VMEM((weight_v.shape[1], tokens), jnp.float32)],
    )(feats, weight_v)


def on_device(inputs, queries, keys, w_value, w_out):
    activ = inputs[0]
    weight_v = w_value[0]
    weight_o = w_out[0]
    length = activ.shape[0]
    col_width = activ.shape[1]
    n_feat = weight_v.shape[0]

    core = lax.axis_index("tc").astype(jnp.int32).reshape(1)
    weight_from_sib = swap(pick_columns(1 - core, weight_o, col_width), "tc")
    other = swap(activ, "ty")
    slot = lax.broadcasted_iota(jnp.int32, (N_Y, 1, 1), 0)
    gathered = jnp.where(slot == lax.axis_index("ty"), activ[None], other[None])
    gathered = lax.all_gather(gathered, ("tz", "tc"), axis=0)
    values = gathered_proj(gathered, weight_v).T

    heads_here = weight_v.shape[1] // HEAD_SIZE
    query_rows = queries[0].reshape(length // LEN, LEN, heads_here, HEAD_SIZE)
    key_rows = keys[0].reshape(length // LEN, LEN, heads_here, HEAD_SIZE)
    value_rows = values.reshape(length // LEN, LEN, heads_here, HEAD_SIZE)
    scores = jnp.einsum(
        "bqhd,bkhd->bhqk", query_rows, key_rows, preferred_element_type=jnp.float32
    ) / jnp.sqrt(jnp.float32(HEAD_SIZE))
    rows = lax.broadcasted_iota(jnp.int32, (LEN, LEN), 0)
    cols = lax.broadcasted_iota(jnp.int32, (LEN, LEN), 1)
    scores = jnp.where((cols <= rows)[None, None], scores, jnp.float32(-1e30))
    top = jnp.max(scores, axis=-1, keepdims=True)
    expo = jnp.exp(scores - top)
    probs = (expo / jnp.sum(expo, axis=-1, keepdims=True)).astype(jnp.bfloat16)
    context = jnp.einsum(
        "bhqk,bkhd->bqhd", probs, value_rows, preferred_element_type=jnp.float32
    ).astype(jnp.bfloat16)
    context = context.reshape(length, heads_here * HEAD_SIZE)

    part = out_proj(core, context, swap(context, "tc"), weight_from_sib, weight_o, col_width)
    part = part.reshape(N_Z, N_Y, length, col_width)
    part = lax.psum_scatter(part, "tz", scatter_dimension=0, tiled=False)
    y_index = lax.axis_index("ty")
    keep = lax.dynamic_index_in_dim(part, y_index, 0, keepdims=False)
    send = lax.dynamic_index_in_dim(part, 1 - y_index, 0, keepdims=False)
    keep = (keep.astype(jnp.float32) + activ.astype(jnp.float32)).astype(jnp.bfloat16)
    across = lax.ppermute(send, ("section", "ty"), [(i, 3 - i) for i in range(4)])
    result = swap(keep, "section").astype(jnp.float32) + across.astype(jnp.float32)
    return result.astype(jnp.bfloat16)[None]


def solution(mesh):
    n_sec, n_dp, n_t = mesh.devices.shape
    sub = Mesh(
        mesh.devices.reshape(n_sec, n_dp, N_Z, N_Y, N_C),
        ("section", "dp", "tz", "ty", "tc"),
    )
    spec = P("section", "dp", ("tz", "ty", "tc"))
    return jax.shard_map(
        on_device,
        mesh=sub,
        in_specs=(
            spec,
            spec,
            spec,
            P("section", None, ("tz", "ty", "tc")),
            P("section", ("tz", "ty", "tc"), None),
        ),
        out_specs=spec,
        check_vma=False,
    )
```

```python
import jax
import jax.numpy as jnp
from jax import lax
from jax.experimental import pallas as pl
from jax.experimental.pallas import tpu as pltpu
from jax.sharding import Mesh
from jax.sharding import PartitionSpec as P

HEAD_SIZE = 128
LEN = 256
N_Z, N_Y, N_C = 8, 2, 2
GROUPS_PER_STEP = 8
Z_PER_STEP = 2


def swap(value, axis):
    return lax.ppermute(value, axis, [(0, 1), (1, 0)])


def column_spec(inner, width, step, k):
    return pl.BlockSpec((inner, width), lambda i, c: (0, N_C * (i * step + k) + c[0]))


def pick_kernel(sel_ref, *refs):
    w_refs, o_ref = refs[:-1], refs[-1]
    for k, w_ref in enumerate(w_refs):
        o_ref[k] = w_ref[...]


def pick_columns(sel, weight_o, width):
    inner = weight_o.shape[0]
    n_groups = weight_o.shape[1] // (N_C * width)
    step = GROUPS_PER_STEP
    return pl.pallas_call(
        pick_kernel,
        out_shape=jax.ShapeDtypeStruct((n_groups, inner, width), weight_o.dtype),
        grid_spec=pltpu.PrefetchScalarGridSpec(
            num_scalar_prefetch=1,
            grid=(n_groups // step,),
            in_specs=[column_spec(inner, width, step, k) for k in range(step)],
            out_specs=pl.BlockSpec((step, inner, width), lambda i, c: (i, 0, 0)),
        ),
    )(sel, *([weight_o] * step))


def out_proj_kernel(core_ref, ctx_ref, ctx_sib_ref, w_sib_ref, *refs):
    w_refs, o_ref = refs[:-1], refs[-1]
    ctx = ctx_ref[...]
    ctx_sib = ctx_sib_ref[...]
    for k, w_ref in enumerate(w_refs):
        d = jnp.dot(ctx, w_ref[...], preferred_element_type=jnp.float32)
        d = d + jnp.dot(ctx_sib, w_sib_ref[k], preferred_element_type=jnp.float32)
        o_ref[k] = d.astype(jnp.bfloat16)


def out_proj(core, context, context_sib, weight_sib, weight_o, width):
    tokens, inner = context.shape
    n_groups = weight_o.shape[1] // (N_C * width)
    step = GROUPS_PER_STEP
    return pl.pallas_call(
        out_proj_kernel,
        out_shape=jax.ShapeDtypeStruct((n_groups, tokens, width), jnp.bfloat16),
        grid_spec=pltpu.PrefetchScalarGridSpec(
            num_scalar_prefetch=1,
            grid=(n_groups // step,),
            in_specs=[
                pl.BlockSpec((tokens, inner), lambda i, c: (0, 0)),
                pl.BlockSpec((tokens, inner), lambda i, c: (0, 0)),
                pl.BlockSpec((step, inner, width), lambda i, c: (i, 0, 0)),
            ]
            + [column_spec(inner, width, step, k) for k in range(step)],
            out_specs=pl.BlockSpec((step, tokens, width), lambda i, c: (i, 0, 0)),
        ),
    )(core, context, context_sib, weight_sib, *([weight_o] * step))


def gathered_proj_kernel(f_ref, w_ref, o_ref, acc_ref):
    width = f_ref.shape[-1]

    @pl.when(pl.program_id(0) == 0)
    def _():
        acc_ref[...] = jnp.zeros(acc_ref.shape, acc_ref.dtype)

    acc = acc_ref[...]
    for z in range(Z_PER_STEP):
        for c in range(N_C):
            for y in range(N_Y):
                slot = (z * N_C + c) * N_Y + y
                row = ((z * N_Y + y) * N_C + c) * width
                acc = acc + lax.dot_general(
                    w_ref[row:row + width, :],
                    f_ref[slot],
                    (((0,), (1,)), ((), ())),
                    preferred_element_type=jnp.float32,
                )
    acc_ref[...] = acc

    @pl.when(pl.program_id(0) == pl.num_programs(0) - 1)
    def _():
        o_ref[...] = acc.astype(o_ref.dtype)


def gathered_proj(feats, weight_v):
    tokens, width = feats.shape[-2:]
    feats = feats.reshape(-1, tokens, width)
    step = Z_PER_STEP * N_C * N_Y
    return pl.pallas_call(
        gathered_proj_kernel,
        out_shape=jax.ShapeDtypeStruct((weight_v.shape[1], tokens), jnp.bfloat16),
        grid=(N_Z // Z_PER_STEP,),
        in_specs=[
            pl.BlockSpec((step, tokens, width), lambda i: (i, 0, 0)),
            pl.BlockSpec((step * width, weight_v.shape[1]), lambda i: (i, 0)),
        ],
        out_specs=pl.BlockSpec((weight_v.shape[1], tokens), lambda i: (0, 0)),
        scratch_shapes=[pltpu.VMEM((weight_v.shape[1], tokens), jnp.float32)],
    )(feats, weight_v)


def on_device(inputs, queries, keys, w_value, w_out):
    activ = inputs[0]
    weight_v = w_value[0]
    weight_o = w_out[0]
    length = activ.shape[0]
    col_width = activ.shape[1]
    n_feat = weight_v.shape[0]

    core = lax.axis_index("tc").astype(jnp.int32).reshape(1)
    weight_from_sib = swap(pick_columns(1 - core, weight_o, col_width), "tc")
    y_first = lax.axis_index("ty") == 0
    other = swap(activ, "ty")
    gathered = jnp.stack([jnp.where(y_first, activ, other), jnp.where(y_first, other, activ)])
    gathered = lax.all_gather(gathered, ("tz", "tc"), axis=0)
    values = gathered_proj(gathered, weight_v).T

    heads_here = weight_v.shape[1] // HEAD_SIZE
    query_rows = queries[0].reshape(length // LEN, LEN, heads_here, HEAD_SIZE)
    key_rows = keys[0].reshape(length // LEN, LEN, heads_here, HEAD_SIZE)
    value_rows = values.reshape(length // LEN, LEN, heads_here, HEAD_SIZE)
    scores = jnp.einsum(
        "bqhd,bkhd->bhqk", query_rows, key_rows, preferred_element_type=jnp.float32
    ) / jnp.sqrt(jnp.float32(HEAD_SIZE))
    rows = lax.broadcasted_iota(jnp.int32, (LEN, LEN), 0)
    cols = lax.broadcasted_iota(jnp.int32, (LEN, LEN), 1)
    scores = jnp.where((cols <= rows)[None, None], scores, jnp.float32(-1e30))
    top = jnp.max(scores, axis=-1, keepdims=True)
    expo = jnp.exp(scores - top)
    probs = (expo / jnp.sum(expo, axis=-1, keepdims=True)).astype(jnp.bfloat16)
    context = jnp.einsum(
        "bhqk,bkhd->bqhd", probs, value_rows, preferred_element_type=jnp.float32
    ).astype(jnp.bfloat16)
    context = context.reshape(length, heads_here * HEAD_SIZE)

    part = out_proj(core, context, swap(context, "tc"), weight_from_sib, weight_o, col_width)
    part = part.reshape(N_Z, N_Y, length, col_width)
    part = lax.psum_scatter(part, "tz", scatter_dimension=0, tiled=False)
    y_index = lax.axis_index("ty")
    keep = lax.dynamic_index_in_dim(part, y_index, 0, keepdims=False)
    send = lax.dynamic_index_in_dim(part, 1 - y_index, 0, keepdims=False)
    keep = (keep.astype(jnp.float32) + activ.astype(jnp.float32)).astype(jnp.bfloat16)
    across = lax.ppermute(send, ("section", "ty"), [(i, 3 - i) for i in range(4)])
    result = swap(keep, "section").astype(jnp.float32) + across.astype(jnp.float32)
    return result.astype(jnp.bfloat16)[None]


def solution(mesh):
    n_sec, n_dp, n_t = mesh.devices.shape
    sub = Mesh(
        mesh.devices.reshape(n_sec, n_dp, N_Z, N_Y, N_C),
        ("section", "dp", "tz", "ty", "tc"),
    )
    spec = P("section", "dp", ("tz", "ty", "tc"))
    return jax.shard_map(
        on_device,
        mesh=sub,
        in_specs=(
            spec,
            spec,
            spec,
            P("section", None, ("tz", "ty", "tc")),
            P("section", ("tz", "ty", "tc"), None),
        ),
        out_specs=spec,
        check_vma=False,
    )
```

```python
import jax
import jax.numpy as jnp
from jax import lax
from jax.experimental import pallas as pl
from jax.experimental.pallas import tpu as pltpu
from jax.sharding import Mesh
from jax.sharding import PartitionSpec as P

HEAD_SIZE = 128
LEN = 256
N_Z, N_Y, N_C = 8, 2, 2
GROUPS_PER_STEP = 16
Z_PER_STEP = 4


def swap(value, axis):
    return lax.ppermute(value, axis, [(0, 1), (1, 0)])


def column_spec(inner, width, step, k):
    return pl.BlockSpec((inner, width), lambda i, c: (0, N_C * (i * step + k) + c[0]))


def pick_kernel(sel_ref, *refs):
    w_refs, o_ref = refs[:-1], refs[-1]
    for k, w_ref in enumerate(w_refs):
        o_ref[k] = w_ref[...]


def pick_columns(sel, weight_o, width):
    inner = weight_o.shape[0]
    n_groups = weight_o.shape[1] // (N_C * width)
    step = GROUPS_PER_STEP
    return pl.pallas_call(
        pick_kernel,
        out_shape=jax.ShapeDtypeStruct((n_groups, inner, width), weight_o.dtype),
        grid_spec=pltpu.PrefetchScalarGridSpec(
            num_scalar_prefetch=1,
            grid=(n_groups // step,),
            in_specs=[column_spec(inner, width, step, k) for k in range(step)],
            out_specs=pl.BlockSpec((step, inner, width), lambda i, c: (i, 0, 0)),
        ),
    )(sel, *([weight_o] * step))


def out_proj_kernel(core_ref, ctx_ref, ctx_sib_ref, w_sib_ref, *refs):
    w_refs, o_ref = refs[:-1], refs[-1]
    ctx = ctx_ref[...]
    ctx_sib = ctx_sib_ref[...]
    for k, w_ref in enumerate(w_refs):
        d = jnp.dot(ctx, w_ref[...], preferred_element_type=jnp.float32)
        d = d + jnp.dot(ctx_sib, w_sib_ref[k], preferred_element_type=jnp.float32)
        o_ref[k] = d.astype(jnp.bfloat16)


def out_proj(core, context, context_sib, weight_sib, weight_o, width):
    tokens, inner = context.shape
    n_groups = weight_o.shape[1] // (N_C * width)
    step = GROUPS_PER_STEP
    return pl.pallas_call(
        out_proj_kernel,
        out_shape=jax.ShapeDtypeStruct((n_groups, tokens, width), jnp.bfloat16),
        grid_spec=pltpu.PrefetchScalarGridSpec(
            num_scalar_prefetch=1,
            grid=(n_groups // step,),
            in_specs=[
                pl.BlockSpec((tokens, inner), lambda i, c: (0, 0)),
                pl.BlockSpec((tokens, inner), lambda i, c: (0, 0)),
                pl.BlockSpec((step, inner, width), lambda i, c: (i, 0, 0)),
            ]
            + [column_spec(inner, width, step, k) for k in range(step)],
            out_specs=pl.BlockSpec((step, tokens, width), lambda i, c: (i, 0, 0)),
        ),
    )(core, context, context_sib, weight_sib, *([weight_o] * step))


def gathered_proj_kernel(f_ref, w_ref, o_ref, acc_ref):
    width = f_ref.shape[-1]

    @pl.when(pl.program_id(0) == 0)
    def _():
        acc_ref[...] = jnp.zeros(acc_ref.shape, acc_ref.dtype)

    acc = acc_ref[...]
    for z in range(Z_PER_STEP):
        for c in range(N_C):
            for y in range(N_Y):
                slot = (z * N_C + c) * N_Y + y
                row = ((z * N_Y + y) * N_C + c) * width
                acc = acc + lax.dot_general(
                    w_ref[row:row + width, :],
                    f_ref[slot],
                    (((0,), (1,)), ((), ())),
                    preferred_element_type=jnp.float32,
                )
    acc_ref[...] = acc

    @pl.when(pl.program_id(0) == pl.num_programs(0) - 1)
    def _():
        o_ref[...] = acc.astype(o_ref.dtype)


def gathered_proj(feats, weight_v):
    tokens, width = feats.shape[-2:]
    feats = feats.reshape(-1, tokens, width)
    step = Z_PER_STEP * N_C * N_Y
    return pl.pallas_call(
        gathered_proj_kernel,
        out_shape=jax.ShapeDtypeStruct((weight_v.shape[1], tokens), jnp.bfloat16),
        grid=(N_Z // Z_PER_STEP,),
        in_specs=[
            pl.BlockSpec((step, tokens, width), lambda i: (i, 0, 0)),
            pl.BlockSpec((step * width, weight_v.shape[1]), lambda i: (i, 0)),
        ],
        out_specs=pl.BlockSpec((weight_v.shape[1], tokens), lambda i: (0, 0)),
        scratch_shapes=[pltpu.VMEM((weight_v.shape[1], tokens), jnp.float32)],
    )(feats, weight_v)


def on_device(inputs, queries, keys, w_value, w_out):
    activ = inputs[0]
    weight_v = w_value[0]
    weight_o = w_out[0]
    length = activ.shape[0]
    col_width = activ.shape[1]
    n_feat = weight_v.shape[0]

    core = lax.axis_index("tc").astype(jnp.int32).reshape(1)
    weight_from_sib = swap(pick_columns(1 - core, weight_o, col_width), "tc")
    y_first = lax.axis_index("ty") == 0
    other = swap(activ, "ty")
    gathered = jnp.stack([jnp.where(y_first, activ, other), jnp.where(y_first, other, activ)])
    gathered = lax.all_gather(gathered, ("tz", "tc"), axis=0)
    values = gathered_proj(gathered, weight_v).T

    heads_here = weight_v.shape[1] // HEAD_SIZE
    query_rows = queries[0].reshape(length // LEN, LEN, heads_here, HEAD_SIZE)
    key_rows = keys[0].reshape(length // LEN, LEN, heads_here, HEAD_SIZE)
    value_rows = values.reshape(length // LEN, LEN, heads_here, HEAD_SIZE)
    scores = jnp.einsum(
        "bqhd,bkhd->bhqk", query_rows, key_rows, preferred_element_type=jnp.float32
    ) / jnp.sqrt(jnp.float32(HEAD_SIZE))
    rows = lax.broadcasted_iota(jnp.int32, (LEN, LEN), 0)
    cols = lax.broadcasted_iota(jnp.int32, (LEN, LEN), 1)
    scores = jnp.where((cols <= rows)[None, None], scores, jnp.float32(-1e30))
    top = jnp.max(scores, axis=-1, keepdims=True)
    expo = jnp.exp(scores - top)
    probs = (expo / jnp.sum(expo, axis=-1, keepdims=True)).astype(jnp.bfloat16)
    context = jnp.einsum(
        "bhqk,bkhd->bqhd", probs, value_rows, preferred_element_type=jnp.float32
    ).astype(jnp.bfloat16)
    context = context.reshape(length, heads_here * HEAD_SIZE)

    part = out_proj(core, context, swap(context, "tc"), weight_from_sib, weight_o, col_width)
    part = part.reshape(N_Z, N_Y, length, col_width)
    part = lax.psum_scatter(part, "tz", scatter_dimension=0, tiled=False)
    y_index = lax.axis_index("ty")
    keep = lax.dynamic_index_in_dim(part, y_index, 0, keepdims=False)
    send = lax.dynamic_index_in_dim(part, 1 - y_index, 0, keepdims=False)
    keep = (keep.astype(jnp.float32) + activ.astype(jnp.float32)).astype(jnp.bfloat16)
    across = lax.ppermute(send, ("section", "ty"), [(i, 3 - i) for i in range(4)])
    result = swap(keep, "section").astype(jnp.float32) + across.astype(jnp.float32)
    return result.astype(jnp.bfloat16)[None]


def solution(mesh):
    n_sec, n_dp, n_t = mesh.devices.shape
    sub = Mesh(
        mesh.devices.reshape(n_sec, n_dp, N_Z, N_Y, N_C),
        ("section", "dp", "tz", "ty", "tc"),
    )
    spec = P("section", "dp", ("tz", "ty", "tc"))
    return jax.shard_map(
        on_device,
        mesh=sub,
        in_specs=(
            spec,
            spec,
            spec,
            P("section", None, ("tz", "ty", "tc")),
            P("section", ("tz", "ty", "tc"), None),
        ),
        out_specs=spec,
        check_vma=False,
    )
```
